256 devices in a mesh: axial: 16 (over x_lo, y, core), azim: 16 (over z, x_hi).
Axes of the slice: x: 4 (x_hi: 2, x_lo: 2; x = x_hi * 2 + x_lo), y: 4, z: 8, core: 2. Of those that a mesh axis runs over, the one named last changes fastest.
Arguments:
- coil_density: float32 [512, 256, 128], P('azim', 'axial'), may hold values from -6 to 6
- coil_mask: int32 [512, 256, 128], P('azim', 'axial'), may hold values 0 or 1
- drive: float32 [2], replicated, may hold values from 0.5 to 2
- potential: float32 [512, 256, 128], P('azim', 'axial'), may hold values from -6 to 6
- tile_weight: float32 [512, 64, 64], P('azim'), may hold values from -0.75 to 0.75
- relay_owner: int32 [2, 512, 16], P(None, 'azim', 'axial'), may hold values from 0 to 2
- relay_slot: int32 [2, 512, 16], P(None, 'azim', 'axial'), may hold values from 0 to 31, as said below
- velocity: float32 [512, 256, 128], P('azim', 'axial'), may hold values from -3 to 3
- strain: float32 [512, 256, 128], P('azim', 'axial'), may hold values from -3 to 3
- plastic: float32 [512, 256, 128], P('azim', 'axial'), may hold values from -0.6 to 0.6
Outputs:
- field_out: float32 [512, 256, 128], P('azim', 'axial')
- velocity_out: float32 [512, 256, 128], P('azim', 'axial')
- strain_out: float32 [512, 256, 128], P('azim', 'axial')
- plastic_out: float32 [512, 256, 128], P('azim', 'axial')
The draws below stay inside these ranges and needn't reach their ends.
Inputs may be any that keep to these rules, and one draw needn't show every extreme that they name: `relay_slot`: for each step and axial block, the values over the 32 azimuthal cells of one sector are a permutation of 0 to 31.
All inputs are finite; a program needn't handle non-finite values. No bound on the sum of `coil_mask` on one device may be relied on, other than what follows from the above.
Results may differ from the reference program's by a relative error of at most 0.00011.
Values sent between devices are 32-bit elements; how exact they have to be, the bound alone decides.
No kernel may reach another device: no remote copies, remote signals or barrier semaphores. Data moves between devices by JAX's collectives and lax.ppermute only.
A program may use at most 64 MiB of HBM per device.

```python
import math
import jax
import jax.numpy as jnp
from jax import lax

NA = 512
R = 128
WR = 64
CZ = 16
STEPS = 2
SWEEPS = 3
NZ = 256
ZBLOCKS = 16
N_AXIAL = 16
N_AZIM = 16


def draw_relay_slot(key, part):
    local_count = NA // N_AZIM
    scores = jax.random.randint(key, (STEPS, N_AZIM, ZBLOCKS, local_count), 0, 1 << 20)
    scores = scores * local_count + jnp.arange(local_count, dtype=jnp.int32)
    ranking = jnp.argsort(scores, axis=-1).astype(jnp.int32)
    return jnp.transpose(ranking, (0, 1, 3, 2)).reshape(STEPS, NA, ZBLOCKS).astype(jnp.int32)


def place_ends(drawn, stream_key, smallest, high):
    dims = drawn.shape
    index_at = [jax.random.randint(jax.random.fold_in(stream_key, axis), (), 0, dims[axis]) for axis in range(len(dims))]
    drawn = drawn.at[tuple(index_at)].set(smallest)
    longest = dims.index(max(dims))
    index_at[longest] = (index_at[longest] + 1) % dims[longest]
    return drawn.at[tuple(index_at)].set(high)


def levels(rng, dims, cuts, low, largest):
    loudness = 1.0
    for position, parts in cuts:
        steps = jax.random.uniform(jax.random.fold_in(jax.random.fold_in(rng, 6), position), (parts,), jnp.float32, low / len(cuts), largest / len(cuts))
        loudness = loudness * jnp.repeat(jnp.exp(steps), dims[position] // parts).reshape((-1,) + (1,) * (len(dims) - 1 - position))
    return loudness


def bell_draw(rng, shape, scale, most, split=(), held_as=jnp.bfloat16):
    entries = jax.random.normal(rng, shape, jnp.float32) * scale
    if len(split) > 0:
        entries = levels(rng, shape, split, -0.22, 0.18) * entries
    return jnp.clip(entries, min=-most, max=most).astype(held_as)


def setup_inputs(seed: int = 0) -> dict:
    keys = jax.random.split(jax.random.key(seed), 11)
    return {
        "coil_density": bell_draw(keys[0], (NA, NZ, R), 1.0, 6.0, ((0, 16), (1, 16)), jnp.float32),
        "coil_mask": place_ends((jax.random.randint(keys[1], (NA, NZ, R), 0, 3) < 1).astype(jnp.int32), jax.random.fold_in(keys[1], 1), 0, 1),
        "drive": jnp.clip(jnp.exp(jax.random.uniform(keys[2], (STEPS,), jnp.float32, math.log(0.5), math.log(2.0))), 0.5, 2.0),
        "potential": bell_draw(keys[3], (NA, NZ, R), 1.0, 6.0, ((0, 16), (1, 16)), jnp.float32),
        "tile_weight": bell_draw(keys[4], (NA, WR, WR), WR ** -0.5, 0.75, ((0, 16),), jnp.float32),
        "relay_owner": place_ends(jax.random.randint(keys[5], (STEPS, NA, ZBLOCKS), 0, 3), jax.random.fold_in(keys[5], 1), 0, 2).astype(jnp.int32),
        "relay_slot": draw_relay_slot(jax.random.fold_in(keys[10], 71), 0),
        "velocity": bell_draw(keys[7], (NA, NZ, 2 * WR), 0.5, 3.0, ((0, 16), (1, 16)), jnp.float32),
        "strain": bell_draw(keys[8], (NA, NZ, 2 * WR), 0.5, 3.0, ((0, 16), (1, 16)), jnp.float32),
        "plastic": bell_draw(keys[9], (NA, NZ, 2 * WR), 0.1, 0.6, ((0, 16), (1, 16)), jnp.float32),
    }


HIGH = lax.Precision.HIGHEST
KAPPA = 2.0
AIR_TERM = 0.05
R_CORE = 16.0
MU_COIL = 1.0
FORCE_K = 1.0
E_MOD = 1.0
YIELD_ZERO = 0.5
HARDEN = 0.3
TIME_STEP = 0.5
STIFFNESS = 0.5
DAMPING = 0.9


def harmonic_table(azimuth, harmonic, count_all):
    half_count = count_all // 2
    orders = jnp.where(harmonic <= half_count, harmonic, harmonic - half_count)
    phases = (azimuth[:, None] * orders[None, :]) % count_all
    angles = phases.astype(jnp.float32) * (2.0 * math.pi / count_all)
    return jnp.where(harmonic[None, :] <= half_count, jnp.cos(angles), jnp.sin(angles))


def harmonic_weight(harmonic, count_all):
    half_count = count_all // 2
    edge_mode = (harmonic == 0) | (harmonic == half_count)
    return jnp.where(edge_mode, 1.0 / count_all, 2.0 / count_all).astype(jnp.float32)


def harmonic_order(harmonic, count_all):
    half_count = count_all // 2
    return jnp.where(harmonic <= half_count, harmonic, harmonic - half_count).astype(jnp.float32)


def radial_profiles(radial_count, band_start, band_width):
    cell_index = jnp.arange(radial_count, dtype=jnp.int32)
    radius = R_CORE + cell_index.astype(jnp.float32)
    inside = (cell_index >= band_start) & (cell_index < band_start + band_width)
    conduct = jnp.where(inside, KAPPA, AIR_TERM).astype(jnp.float32)
    coil_zone = (cell_index < band_start).astype(jnp.float32)
    return radius, conduct, coil_zone


def radial_sum(iterate):
    radial_pad = jnp.pad(iterate, ((0, 0), (0, 0), (1, 1)))
    return radial_pad[:, :, 2:] + radial_pad[:, :, :-2]


def lorentz(padded, previous, conduct, radius, band_start, band_width):
    current_field = padded[:, 1:-1]
    axial_slope = (padded[:, 2:] - padded[:, :-2]) * 0.5
    radial_pad = jnp.pad(current_field, ((0, 0), (0, 0), (1, 1)))
    radial_slope = (radial_pad[:, :, 2:] - radial_pad[:, :, :-2]) * 0.5
    b_axial = radial_slope + current_field / radius
    eddy_current = -conduct * (current_field - previous)
    force_radial = FORCE_K * eddy_current * b_axial
    force_axial = FORCE_K * eddy_current * axial_slope
    return jnp.concatenate([force_radial[..., band_start:band_start + band_width], force_axial[..., band_start:band_start + band_width]], axis=-1)


def plastic_update(load, velocity, strain, plastic):
    trial_stress = E_MOD * (strain - plastic)
    excess = jnp.abs(trial_stress) - YIELD_ZERO
    increment = trial_stress * jnp.maximum(excess, 0.0) / ((E_MOD + HARDEN) * jnp.maximum(jnp.abs(trial_stress), YIELD_ZERO))
    plastic = plastic + increment
    stress = E_MOD * (strain - plastic)
    velocity = DAMPING * velocity + TIME_STEP * (load - STIFFNESS * stress)
    strain = strain + TIME_STEP * velocity
    return velocity, strain, plastic


def relay(tiles, owner, slot, tile_weight):
    local_count = NA // N_AZIM
    grouped = tiles.reshape(N_AZIM, local_count, N_AXIAL, CZ, 2 * WR)
    owner_grid = owner.reshape(N_AZIM, local_count, N_AXIAL)
    slot_grid = slot.reshape(N_AZIM, local_count, N_AXIAL)
    slot_table = (slot_grid[..., None] == jnp.arange(local_count, dtype=jnp.int32)).astype(jnp.float32)
    moved_tiles = []
    for target in range(3):
        chosen = (owner_grid == target).astype(jnp.float32)
        moved_tiles.append(jnp.einsum('sjbcw,sjbp->spbcw', grouped * chosen[..., None, None], slot_table, precision=HIGH))
    zeros_block = jnp.zeros_like(moved_tiles[0][:, :, :1])
    from_below = jnp.concatenate([zeros_block, moved_tiles[2][:, :, :-1]], axis=2)
    from_above = jnp.concatenate([moved_tiles[0][:, :, 1:], zeros_block], axis=2)
    received = (moved_tiles[1] + from_below + from_above).reshape(NA, NZ, 2, WR)
    load = jnp.einsum('aqr,azcr->azcq', tile_weight, received, precision=HIGH)
    return load.reshape(NA, NZ, 2 * WR)


def reference(coil_density, coil_mask, drive, potential, tile_weight, relay_owner, relay_slot, velocity, strain, plastic):
    azimuth = jnp.arange(NA, dtype=jnp.int32)
    forward_table = harmonic_table(azimuth, azimuth, NA)
    inverse_table = (harmonic_table(azimuth, azimuth, NA) * harmonic_weight(azimuth, NA)[None, :]).T
    band_start = R // 4
    radius, conduct, coil_zone = radial_profiles(R, band_start, WR)
    orders = harmonic_order(azimuth, NA)
    diagonal_term = 4.0 + conduct[None, None, :] + (orders[:, None, None] / radius[None, None, :]) ** 2
    field = potential
    for step_index in range(STEPS):
        source = drive[step_index] * coil_density * coil_mask.astype(jnp.float32) * coil_zone
        source_modes = jnp.einsum('ak,azr->kzr', forward_table, source, precision=HIGH)
        field_modes = jnp.einsum('ak,azr->kzr', forward_table, field, precision=HIGH)
        right_side = MU_COIL * source_modes + conduct * field_modes
        iterate = field_modes
        for sweep_index in range(SWEEPS):
            axial_pad = jnp.pad(iterate, ((0, 0), (1, 1), (0, 0)))
            nearby = axial_pad[:, 2:] + axial_pad[:, :-2] + radial_sum(iterate)
            iterate = (right_side + nearby) / diagonal_term
        new_field = jnp.einsum('ka,kzr->azr', inverse_table, iterate, precision=HIGH)
        padded = jnp.pad(new_field, ((0, 0), (1, 1), (0, 0)))
        tiles = lorentz(padded, field, conduct, radius, band_start, WR)
        load = relay(tiles, relay_owner[step_index], relay_slot[step_index], tile_weight)
        velocity, strain, plastic = plastic_update(load, velocity, strain, plastic)
        field = new_field
    return field, velocity, strain, plastic
```

```python
import math

import jax
import jax.numpy as jnp
from jax import lax
from jax.sharding import PartitionSpec as P

STEPS = 2
SWEEPS = 3


HIGH = lax.Precision.HIGHEST
KAPPA = 2.0
AIR_TERM = 0.05
R_CORE = 16.0
MU_COIL = 1.0
FORCE_K = 1.0
E_MOD = 1.0
YIELD_ZERO = 0.5
HARDEN = 0.3
TIME_STEP = 0.5
STIFFNESS = 0.5
DAMPING = 0.9


def with_halo(block, sides, width):
    for axis, dim in sides:
        count = lax.axis_size(axis)
        forward = [(i, i + 1) for i in range(count - 1)]
        backward = [(target, source) for source, target in forward]
        low = lax.ppermute(
            lax.slice_in_dim(block, block.shape[dim] - width, None, axis=dim), axis, forward
        )
        high = lax.ppermute(lax.slice_in_dim(block, 0, width, axis=dim), axis, backward)
        block = jnp.concatenate([low, block, high], axis=dim)
    return block


def shifted(array, axis, by):
    devices = lax.axis_size(axis)
    pairs = [(i, i + by) for i in range(devices) if 0 <= i + by < devices]
    return lax.ppermute(array, axis, pairs)


def harmonic_table(azimuth, harmonic, count_all):
    half_count = count_all // 2
    orders = jnp.where(harmonic <= half_count, harmonic, harmonic - half_count)
    phases = azimuth[:, None] * orders[None, :] % count_all
    angles = phases.astype(jnp.float32) * (2.0 * math.pi / count_all)
    return jnp.where(harmonic[None, :] <= half_count, jnp.cos(angles), jnp.sin(angles))


def harmonic_weight(harmonic, count_all):
    half_count = count_all // 2
    edge_mode = (harmonic == 0) | (harmonic == half_count)
    return jnp.where(edge_mode, 1.0 / count_all, 2.0 / count_all).astype(jnp.float32)


def harmonic_order(harmonic, count_all):
    half_count = count_all // 2
    return jnp.where(harmonic <= half_count, harmonic, harmonic - half_count).astype(jnp.float32)


def radial_profiles(radial_count, band_start, band_width):
    cell_index = jnp.arange(radial_count, dtype=jnp.int32)
    radius = R_CORE + cell_index.astype(jnp.float32)
    inside = (cell_index >= band_start) & (cell_index < band_start + band_width)
    conduct = jnp.where(inside, KAPPA, AIR_TERM).astype(jnp.float32)
    coil_zone = (cell_index < band_start).astype(jnp.float32)
    return (radius, conduct, coil_zone)


def radial_sum(iterate):
    radial_pad = jnp.pad(iterate, ((0, 0), (0, 0), (1, 1)))
    return radial_pad[:, :, 2:] + radial_pad[:, :, :-2]


def lorentz(padded, previous, conduct, radius, band_start, band_width):
    current_field = padded[:, 1:-1]
    axial_slope = (padded[:, 2:] - padded[:, :-2]) * 0.5
    radial_pad = jnp.pad(current_field, ((0, 0), (0, 0), (1, 1)))
    radial_slope = (radial_pad[:, :, 2:] - radial_pad[:, :, :-2]) * 0.5
    b_axial = radial_slope + current_field / radius
    eddy_current = -conduct * (current_field - previous)
    force_radial = FORCE_K * eddy_current * b_axial
    force_axial = FORCE_K * eddy_current * axial_slope
    return jnp.concatenate(
        [
            force_radial[..., band_start : band_start + band_width],
            force_axial[..., band_start : band_start + band_width],
        ],
        axis=-1,
    )


def plastic_update(load, velocity, strain, plastic):
    trial_stress = E_MOD * (strain - plastic)
    excess = jnp.abs(trial_stress) - YIELD_ZERO
    increment = (
        trial_stress
        * jnp.maximum(excess, 0.0)
        / ((E_MOD + HARDEN) * jnp.maximum(jnp.abs(trial_stress), YIELD_ZERO))
    )
    plastic = plastic + increment
    stress = E_MOD * (strain - plastic)
    velocity = DAMPING * velocity + TIME_STEP * (load - STIFFNESS * stress)
    strain = strain + TIME_STEP * velocity
    return (velocity, strain, plastic)


def transform(parts, table):
    flat_shape = parts.shape
    columns_all = parts.reshape(flat_shape[0], -1)
    spread = lax.all_to_all(columns_all, "azim", split_axis=1, concat_axis=0, tiled=True)
    mixed = jnp.dot(table, spread, precision=HIGH, preferred_element_type=jnp.float32)
    joined = lax.all_to_all(mixed, "azim", split_axis=0, concat_axis=1, tiled=True)
    return joined.reshape(flat_shape)


def shards(
    coil_density,
    coil_mask,
    drive,
    potential,
    tile_weight,
    relay_owner,
    relay_slot,
    velocity,
    strain,
    plastic,
):
    local_count, axial_cells, radial_cells = potential.shape
    band_width = tile_weight.shape[1]
    azim_total = local_count * lax.axis_size("azim")
    own_index = lax.axis_index("azim") * local_count + jnp.arange(local_count, dtype=jnp.int32)
    all_index = jnp.arange(azim_total, dtype=jnp.int32)
    band_start = radial_cells // 4
    radius, conduct, coil_zone = radial_profiles(radial_cells, band_start, band_width)
    orders = harmonic_order(own_index, azim_total)
    diagonal_term = (
        4.0 + conduct[None, None, :] + (orders[:, None, None] / radius[None, None, :]) ** 2
    )
    basis = harmonic_table(all_index, all_index, azim_total)
    forward_table = basis.T
    inverse_table = basis * harmonic_weight(all_index, azim_total)[None, :]

    coil = coil_density[..., :band_start] * coil_mask[..., :band_start].astype(jnp.float32)
    modes = transform(jnp.concatenate([potential, coil], axis=-1), forward_table)

    reach = STEPS * SWEEPS + 1
    modes = with_halo(modes, (("axial", 1),), reach)
    field_modes = modes[..., :radial_cells]
    coil_modes = jnp.pad(modes[..., radial_cells:], ((0, 0), (0, 0), (0, radial_cells - band_start)))
    span = axial_cells + 2 * reach
    global_z = lax.axis_index("axial") * axial_cells - reach + jnp.arange(span, dtype=jnp.int32)
    inside = ((global_z >= 0) & (global_z < axial_cells * lax.axis_size("axial")))[None, :, None]

    iterate = field_modes
    kept = []
    for step_index in range(STEPS):
        right_side = MU_COIL * (drive[step_index] * coil_modes) + conduct * iterate
        for sweep_index in range(SWEEPS):
            axial_pad = jnp.pad(iterate, ((0, 0), (1, 1), (0, 0)))
            nearby = axial_pad[:, 2:] + axial_pad[:, :-2] + radial_sum(iterate)
            iterate = jnp.where(inside, (right_side + nearby) / diagonal_term, 0.0)
        kept.append(iterate[:, reach - 1 : reach + axial_cells + 1])
    fields = transform(jnp.concatenate(kept, axis=-1), inverse_table)

    slot_range = jnp.arange(local_count, dtype=jnp.int32)
    previous = potential
    same, upward, downward = [], [], []
    for step_index in range(STEPS):
        padded = fields[..., step_index * radial_cells : (step_index + 1) * radial_cells]
        tiles = lorentz(padded, previous, conduct, radius, band_start, band_width)
        previous = padded[:, 1:-1]
        slot_table = (relay_slot[step_index, :, 0][:, None] == slot_range[None, :]).astype(
            jnp.float32
        )
        owner_now = relay_owner[step_index, :, 0]

        def place(target):
            chosen = (owner_now == target).astype(jnp.float32)
            return jnp.einsum(
                "jcw,jp->pcw", tiles * chosen[:, None, None], slot_table, precision=HIGH
            )

        same.append(place(1))
        upward.append(place(2))
        downward.append(place(0))
    from_below = shifted(jnp.stack(upward), "axial", 1)
    from_above = shifted(jnp.stack(downward), "axial", -1)
    for step_index in range(STEPS):
        received = (same[step_index] + from_below[step_index] + from_above[step_index]).reshape(
            local_count, axial_cells, 2, band_width
        )
        load = jnp.einsum("aqr,azcr->azcq", tile_weight, received, precision=HIGH).reshape(
            local_count, axial_cells, 2 * band_width
        )
        velocity, strain, plastic = plastic_update(load, velocity, strain, plastic)
    return (previous, velocity, strain, plastic)


def solution(mesh):
    placed = (
        P("azim", "axial", None),
        P("azim", "axial", None),
        P(),
        P("azim", "axial", None),
        P("azim", None, None),
        P(None, "azim", "axial"),
        P(None, "azim", "axial"),
        P("azim", "axial", None),
        P("azim", "axial", None),
        P("azim", "axial", None),
    )
    return jax.shard_map(
        shards,
        mesh=mesh,
        in_specs=placed,
        out_specs=(
            P("azim", "axial", None),
            P("azim", "axial", None),
            P("azim", "axial", None),
            P("azim", "axial", None),
        ),
        check_vma=False,
    )
```

```python
import math

import jax
import numpy as np
import jax.numpy as jnp
from jax import lax
from jax.sharding import PartitionSpec as P

STEPS = 2
SWEEPS = 3


HIGH = lax.Precision.HIGHEST
KAPPA = 2.0
AIR_TERM = 0.05
R_CORE = 16.0
MU_COIL = 1.0
FORCE_K = 1.0
E_MOD = 1.0
YIELD_ZERO = 0.5
HARDEN = 0.3
TIME_STEP = 0.5
STIFFNESS = 0.5
DAMPING = 0.9


def with_halo(block, sides, width):
    for axis, dim in sides:
        count = lax.axis_size(axis)
        forward = [(i, i + 1) for i in range(count - 1)]
        backward = [(target, source) for source, target in forward]
        low = lax.ppermute(
            lax.slice_in_dim(block, block.shape[dim] - width, None, axis=dim), axis, forward
        )
        high = lax.ppermute(lax.slice_in_dim(block, 0, width, axis=dim), axis, backward)
        block = jnp.concatenate([low, block, high], axis=dim)
    return block


def shifted(array, axis, by):
    devices = lax.axis_size(axis)
    pairs = [(i, i + by) for i in range(devices) if 0 <= i + by < devices]
    return lax.ppermute(array, axis, pairs)


def harmonic_table(azimuth, harmonic, count_all):
    half_count = count_all // 2
    orders = jnp.where(harmonic <= half_count, harmonic, harmonic - half_count)
    phases = azimuth[:, None] * orders[None, :] % count_all
    angles = phases.astype(jnp.float32) * (2.0 * math.pi / count_all)
    return jnp.where(harmonic[None, :] <= half_count, jnp.cos(angles), jnp.sin(angles))


def harmonic_weight(harmonic, count_all):
    half_count = count_all // 2
    edge_mode = (harmonic == 0) | (harmonic == half_count)
    return jnp.where(edge_mode, 1.0 / count_all, 2.0 / count_all).astype(jnp.float32)


def harmonic_order(harmonic, count_all):
    half_count = count_all // 2
    return jnp.where(harmonic <= half_count, harmonic, harmonic - half_count).astype(jnp.float32)


def radial_profiles(radial_count, band_start, band_width):
    cell_index = jnp.arange(radial_count, dtype=jnp.int32)
    radius = R_CORE + cell_index.astype(jnp.float32)
    inside = (cell_index >= band_start) & (cell_index < band_start + band_width)
    conduct = jnp.where(inside, KAPPA, AIR_TERM).astype(jnp.float32)
    coil_zone = (cell_index < band_start).astype(jnp.float32)
    return (radius, conduct, coil_zone)


def radial_sum(iterate):
    radial_pad = jnp.pad(iterate, ((0, 0), (0, 0), (1, 1)))
    return radial_pad[:, :, 2:] + radial_pad[:, :, :-2]


def lorentz(padded, previous, conduct, radius, band_start, band_width):
    current_field = padded[:, 1:-1]
    axial_slope = (padded[:, 2:] - padded[:, :-2]) * 0.5
    radial_pad = jnp.pad(current_field, ((0, 0), (0, 0), (1, 1)))
    radial_slope = (radial_pad[:, :, 2:] - radial_pad[:, :, :-2]) * 0.5
    b_axial = radial_slope + current_field / radius
    eddy_current = -conduct * (current_field - previous)
    force_radial = FORCE_K * eddy_current * b_axial
    force_axial = FORCE_K * eddy_current * axial_slope
    return jnp.concatenate(
        [
            force_radial[..., band_start : band_start + band_width],
            force_axial[..., band_start : band_start + band_width],
        ],
        axis=-1,
    )


def plastic_update(load, velocity, strain, plastic):
    trial_stress = E_MOD * (strain - plastic)
    excess = jnp.abs(trial_stress) - YIELD_ZERO
    increment = (
        trial_stress
        * jnp.maximum(excess, 0.0)
        / ((E_MOD + HARDEN) * jnp.maximum(jnp.abs(trial_stress), YIELD_ZERO))
    )
    plastic = plastic + increment
    stress = E_MOD * (strain - plastic)
    velocity = DAMPING * velocity + TIME_STEP * (load - STIFFNESS * stress)
    strain = strain + TIME_STEP * velocity
    return (velocity, strain, plastic)


def basis_constant(count_all):
    half_count = count_all // 2
    harmonic = np.arange(count_all)
    orders = np.where(harmonic <= half_count, harmonic, harmonic - half_count)
    phases = (harmonic[:, None] * orders[None, :]) % count_all
    angles = phases.astype(np.float64) * (2.0 * math.pi / count_all)
    table = np.where(harmonic[None, :] <= half_count, np.cos(angles), np.sin(angles))
    return table.astype(np.float32)


def transform(flat, basis, inverse):
    rows, count = flat.shape
    devices = lax.axis_size("azim")
    unit = devices * 128 // math.gcd(rows, 128)
    padded = -(-count // unit) * unit
    flat = jnp.pad(flat, ((0, 0), (0, padded - count)))
    width = padded // devices
    dense = (devices, rows * width // 128, 128)
    blocks = flat.reshape(rows, devices, width).transpose(1, 0, 2).reshape(dense)
    spread = lax.all_to_all(blocks, "azim", 0, 0, tiled=True).reshape(devices * rows, width)
    contract = 1 if inverse else 0
    mixed = lax.dot_general(
        basis, spread, (((contract,), (0,)), ((), ())), precision=HIGH,
        preferred_element_type=jnp.float32,
    )
    joined = lax.all_to_all(mixed.reshape(dense), "azim", 0, 0, tiled=True)
    return joined.reshape(devices, rows, width).transpose(1, 0, 2).reshape(rows, padded)[:, :count]


def lorentz_window(padded, previous, conduct, radius):
    current_field = padded[:, 1:-1]
    axial_slope = (padded[:, 2:] - padded[:, :-2]) * 0.5
    radial_pad = jnp.pad(current_field, ((0, 0), (0, 0), (1, 1)))
    radial_slope = (radial_pad[:, :, 2:] - radial_pad[:, :, :-2]) * 0.5
    b_axial = radial_slope + current_field / radius
    eddy_current = -conduct * (current_field - previous)
    force_radial = FORCE_K * eddy_current * b_axial
    force_axial = FORCE_K * eddy_current * axial_slope
    return jnp.concatenate([force_radial[..., 1:-1], force_axial[..., 1:-1]], axis=-1)


def shards(
    coil_density,
    coil_mask,
    drive,
    potential,
    tile_weight,
    relay_owner,
    relay_slot,
    velocity,
    strain,
    plastic,
):
    local_count, axial_cells, radial_cells = potential.shape
    band_width = tile_weight.shape[1]
    azim_total = local_count * lax.axis_size("azim")
    own_index = lax.axis_index("azim") * local_count + jnp.arange(local_count, dtype=jnp.int32)
    band_start = radial_cells // 4
    radius, conduct, coil_zone = radial_profiles(radial_cells, band_start, band_width)
    orders = harmonic_order(own_index, azim_total)
    diagonal_term = (
        4.0 + conduct[None, None, :] + (orders[:, None, None] / radius[None, None, :]) ** 2
    )
    basis = jnp.asarray(basis_constant(azim_total))

    coil = coil_density[..., :band_start] * coil_mask[..., :band_start].astype(jnp.float32)
    flat = jnp.concatenate(
        [potential.reshape(local_count, -1), coil.reshape(local_count, -1)], axis=1
    )
    modes = transform(flat, basis, inverse=False)
    split_at = axial_cells * radial_cells
    modes = jnp.concatenate(
        [
            modes[:, :split_at].reshape(local_count, axial_cells, radial_cells),
            modes[:, split_at:].reshape(local_count, axial_cells, band_start),
        ],
        axis=-1,
    )

    reach = STEPS * SWEEPS + 1
    modes = with_halo(modes, (("axial", 1),), reach)
    field_modes = modes[..., :radial_cells]
    coil_modes = jnp.pad(modes[..., radial_cells:], ((0, 0), (0, 0), (0, radial_cells - band_start)))
    span = axial_cells + 2 * reach
    global_z = lax.axis_index("axial") * axial_cells - reach + jnp.arange(span, dtype=jnp.int32)
    inside = ((global_z >= 0) & (global_z < axial_cells * lax.axis_size("axial")))[None, :, None]

    weight = harmonic_weight(own_index, azim_total)[:, None, None]
    window = slice(band_start - 1, band_start + band_width + 1)
    iterate = field_modes
    kept = []
    for step_index in range(STEPS):
        right_side = MU_COIL * (drive[step_index] * coil_modes) + conduct * iterate
        for sweep_index in range(SWEEPS):
            axial_pad = jnp.pad(iterate, ((0, 0), (1, 1), (0, 0)))
            nearby = axial_pad[:, 2:] + axial_pad[:, :-2] + radial_sum(iterate)
            iterate = jnp.where(inside, (right_side + nearby) / diagonal_term, 0.0)
        planes = iterate[:, reach - 1 : reach + axial_cells + 1] * weight
        kept.append(planes if step_index == STEPS - 1 else planes[..., window])
    pieces = [piece.shape for piece in kept]
    flat = transform(
        jnp.concatenate([piece.reshape(local_count, -1) for piece in kept], axis=1),
        basis,
        inverse=True,
    )
    fields, offset = [], 0
    for shape in pieces:
        size = math.prod(shape[1:])
        fields.append(flat[:, offset : offset + size].reshape(shape))
        offset += size

    slot_range = jnp.arange(local_count, dtype=jnp.int32)
    previous = potential[..., window]
    same, upward, downward = [], [], []
    for step_index in range(STEPS):
        padded = fields[step_index]
        if step_index == STEPS - 1:
            field_out = padded[:, 1:-1]
            padded = padded[..., window]
        tiles = lorentz_window(padded, previous, conduct[window], radius[window])
        previous = padded[:, 1:-1]
        slot_table = (relay_slot[step_index, :, 0][:, None] == slot_range[None, :]).astype(
            jnp.float32
        )
        owner_now = relay_owner[step_index, :, 0]

        def place(target):
            chosen = (owner_now == target).astype(jnp.float32)
            return jnp.einsum(
                "jcw,jp->pcw", tiles * chosen[:, None, None], slot_table, precision=HIGH
            )

        same.append(place(1))
        upward.append(place(2))
        downward.append(place(0))
    from_below = shifted(jnp.stack(upward), "axial", 1)
    from_above = shifted(jnp.stack(downward), "axial", -1)
    for step_index in range(STEPS):
        received = (same[step_index] + from_below[step_index] + from_above[step_index]).reshape(
            local_count, axial_cells, 2, band_width
        )
        load = jnp.einsum("aqr,azcr->azcq", tile_weight, received, precision=HIGH).reshape(
            local_count, axial_cells, 2 * band_width
        )
        velocity, strain, plastic = plastic_update(load, velocity, strain, plastic)
    return (field_out, velocity, strain, plastic)


def solution(mesh):
    placed = (
        P("azim", "axial", None),
        P("azim", "axial", None),
        P(),
        P("azim", "axial", None),
        P("azim", None, None),
        P(None, "azim", "axial"),
        P(None, "azim", "axial"),
        P("azim", "axial", None),
        P("azim", "axial", None),
        P("azim", "axial", None),
    )
    return jax.shard_map(
        shards,
        mesh=mesh,
        in_specs=placed,
        out_specs=(
            P("azim", "axial", None),
            P("azim", "axial", None),
            P("azim", "axial", None),
            P("azim", "axial", None),
        ),
        check_vma=False,
    )
```

```python
import math

import jax
import numpy as np
import jax.numpy as jnp
from jax import lax
from jax.sharding import PartitionSpec as P

STEPS = 2
SWEEPS = 3


HIGH = lax.Precision.HIGHEST
KAPPA = 2.0
AIR_TERM = 0.05
R_CORE = 16.0
MU_COIL = 1.0
FORCE_K = 1.0
E_MOD = 1.0
YIELD_ZERO = 0.5
HARDEN = 0.3
TIME_STEP = 0.5
STIFFNESS = 0.5
DAMPING = 0.9


def with_halo(block, sides, width):
    for axis, dim in sides:
        count = lax.axis_size(axis)
        forward = [(i, i + 1) for i in range(count - 1)]
        backward = [(target, source) for source, target in forward]
        low = lax.ppermute(
            lax.slice_in_dim(block, block.shape[dim] - width, None, axis=dim), axis, forward
        )
        high = lax.ppermute(lax.slice_in_dim(block, 0, width, axis=dim), axis, backward)
        block = jnp.concatenate([low, block, high], axis=dim)
    return block


def shifted(array, axis, by):
    devices = lax.axis_size(axis)
    pairs = [(i, i + by) for i in range(devices) if 0 <= i + by < devices]
    return lax.ppermute(array, axis, pairs)


def harmonic_table(azimuth, harmonic, count_all):
    half_count = count_all // 2
    orders = jnp.where(harmonic <= half_count, harmonic, harmonic - half_count)
    phases = azimuth[:, None] * orders[None, :] % count_all
    angles = phases.astype(jnp.float32) * (2.0 * math.pi / count_all)
    return jnp.where(harmonic[None, :] <= half_count, jnp.cos(angles), jnp.sin(angles))


def harmonic_weight(harmonic, count_all):
    half_count = count_all // 2
    edge_mode = (harmonic == 0) | (harmonic == half_count)
    return jnp.where(edge_mode, 1.0 / count_all, 2.0 / count_all).astype(jnp.float32)


def harmonic_order(harmonic, count_all):
    half_count = count_all // 2
    return jnp.where(harmonic <= half_count, harmonic, harmonic - half_count).astype(jnp.float32)


def radial_profiles(radial_count, band_start, band_width):
    cell_index = jnp.arange(radial_count, dtype=jnp.int32)
    radius = R_CORE + cell_index.astype(jnp.float32)
    inside = (cell_index >= band_start) & (cell_index < band_start + band_width)
    conduct = jnp.where(inside, KAPPA, AIR_TERM).astype(jnp.float32)
    coil_zone = (cell_index < band_start).astype(jnp.float32)
    return (radius, conduct, coil_zone)


def radial_sum(iterate):
    radial_pad = jnp.pad(iterate, ((0, 0), (0, 0), (1, 1)))
    return radial_pad[:, :, 2:] + radial_pad[:, :, :-2]


def lorentz(padded, previous, conduct, radius, band_start, band_width):
    current_field = padded[:, 1:-1]
    axial_slope = (padded[:, 2:] - padded[:, :-2]) * 0.5
    radial_pad = jnp.pad(current_field, ((0, 0), (0, 0), (1, 1)))
    radial_slope = (radial_pad[:, :, 2:] - radial_pad[:, :, :-2]) * 0.5
    b_axial = radial_slope + current_field / radius
    eddy_current = -conduct * (current_field - previous)
    force_radial = FORCE_K * eddy_current * b_axial
    force_axial = FORCE_K * eddy_current * axial_slope
    return jnp.concatenate(
        [
            force_radial[..., band_start : band_start + band_width],
            force_axial[..., band_start : band_start + band_width],
        ],
        axis=-1,
    )


def plastic_update(load, velocity, strain, plastic):
    trial_stress = E_MOD * (strain - plastic)
    excess = jnp.abs(trial_stress) - YIELD_ZERO
    increment = (
        trial_stress
        * jnp.maximum(excess, 0.0)
        / ((E_MOD + HARDEN) * jnp.maximum(jnp.abs(trial_stress), YIELD_ZERO))
    )
    plastic = plastic + increment
    stress = E_MOD * (strain - plastic)
    velocity = DAMPING * velocity + TIME_STEP * (load - STIFFNESS * stress)
    strain = strain + TIME_STEP * velocity
    return (velocity, strain, plastic)


def basis_constant(count_all):
    half_count = count_all // 2
    harmonic = np.arange(count_all)
    orders = np.where(harmonic <= half_count, harmonic, harmonic - half_count)
    phases = (harmonic[:, None] * orders[None, :]) % count_all
    angles = phases.astype(np.float64) * (2.0 * math.pi / count_all)
    table = np.where(harmonic[None, :] <= half_count, np.cos(angles), np.sin(angles))
    return table.astype(np.float32)


def transform(flat, basis, inverse):
    rows, count = flat.shape
    devices = lax.axis_size("azim")
    unit = devices * 128 // math.gcd(rows, 128)
    padded = -(-count // unit) * unit
    flat = jnp.pad(flat, ((0, 0), (0, padded - count)))
    width = padded // devices
    dense = (devices, rows * width // 128, 128)
    blocks = flat.reshape(rows, devices, width).transpose(1, 0, 2).reshape(dense)
    spread = lax.all_to_all(blocks, "azim", 0, 0, tiled=True).reshape(devices * rows, width)
    contract = 1 if inverse else 0
    mixed = lax.dot_general(
        basis, spread, (((contract,), (0,)), ((), ())), precision=HIGH,
        preferred_element_type=jnp.float32,
    )
    joined = lax.all_to_all(mixed.reshape(dense), "azim", 0, 0, tiled=True)
    return joined.reshape(devices, rows, width).transpose(1, 0, 2).reshape(rows, padded)[:, :count]


def lorentz_window(padded, previous, conduct, radius):
    current_field = padded[:, 1:-1]
    axial_slope = (padded[:, 2:] - padded[:, :-2]) * 0.5
    radial_pad = jnp.pad(current_field, ((0, 0), (0, 0), (1, 1)))
    radial_slope = (radial_pad[:, :, 2:] - radial_pad[:, :, :-2]) * 0.5
    b_axial = radial_slope + current_field / radius
    eddy_current = -conduct * (current_field - previous)
    force_radial = FORCE_K * eddy_current * b_axial
    force_axial = FORCE_K * eddy_current * axial_slope
    return jnp.concatenate([force_radial[..., 1:-1], force_axial[..., 1:-1]], axis=-1)


def shards(
    coil_density,
    coil_mask,
    drive,
    potential,
    tile_weight,
    relay_owner,
    relay_slot,
    velocity,
    strain,
    plastic,
):
    local_count, axial_cells, radial_cells = potential.shape
    band_width = tile_weight.shape[1]
    azim_total = local_count * lax.axis_size("azim")
    own_index = lax.axis_index("azim") * local_count + jnp.arange(local_count, dtype=jnp.int32)
    band_start = radial_cells // 4
    radius, conduct, coil_zone = radial_profiles(radial_cells, band_start, band_width)
    orders = harmonic_order(own_index, azim_total)
    diagonal_term = (
        4.0 + conduct[None, None, :] + (orders[:, None, None] / radius[None, None, :]) ** 2
    )
    basis = jnp.asarray(basis_constant(azim_total))

    coil = coil_density[..., :band_start] * coil_mask[..., :band_start].astype(jnp.float32)
    flat = jnp.concatenate(
        [potential.reshape(local_count, -1), coil.reshape(local_count, -1)], axis=1
    )
    modes = transform(flat, basis, inverse=False)
    split_at = axial_cells * radial_cells
    modes = jnp.concatenate(
        [
            modes[:, :split_at].reshape(local_count, axial_cells, radial_cells),
            modes[:, split_at:].reshape(local_count, axial_cells, band_start),
        ],
        axis=-1,
    )

    reach = STEPS * SWEEPS + 1
    modes = with_halo(modes, (("axial", 1),), reach)
    field_modes = modes[..., :radial_cells]
    coil_modes = jnp.pad(modes[..., radial_cells:], ((0, 0), (0, 0), (0, radial_cells - band_start)))
    span = axial_cells + 2 * reach
    global_z = lax.axis_index("axial") * axial_cells - reach + jnp.arange(span, dtype=jnp.int32)
    inside = ((global_z >= 0) & (global_z < axial_cells * lax.axis_size("axial")))[None, :, None]

    weight = harmonic_weight(own_index, azim_total)[:, None, None]
    window = slice(band_start - 1, band_start + band_width + 1)
    iterate = field_modes
    kept = []
    for step_index in range(STEPS):
        right_side = MU_COIL * (drive[step_index] * coil_modes) + conduct * iterate
        for sweep_index in range(SWEEPS):
            axial_pad = jnp.pad(iterate, ((0, 0), (1, 1), (0, 0)))
            nearby = axial_pad[:, 2:] + axial_pad[:, :-2] + radial_sum(iterate)
            iterate = jnp.where(inside, (right_side + nearby) / diagonal_term, 0.0)
        planes = iterate[:, reach - 1 : reach + axial_cells + 1] * weight
        kept.append(planes if step_index == STEPS - 1 else planes[..., window])
    pieces = [piece.shape for piece in kept]
    flat = transform(
        jnp.concatenate([piece.reshape(local_count, -1) for piece in kept], axis=1),
        basis,
        inverse=True,
    )
    fields, offset = [], 0
    for shape in pieces:
        size = math.prod(shape[1:])
        fields.append(flat[:, offset : offset + size].reshape(shape))
        offset += size

    previous = potential[..., window]
    tiles = []
    for step_index in range(STEPS):
        padded = fields[step_index]
        if step_index == STEPS - 1:
            field_out = padded[:, 1:-1]
            padded = padded[..., window]
        tiles.append(lorentz_window(padded, previous, conduct[window], radius[window]))
        previous = padded[:, 1:-1]
    tiles = jnp.stack(tiles)

    slot_range = jnp.arange(local_count, dtype=jnp.int32)
    slot_table = relay_slot[:, :, 0][:, :, None] == slot_range[None, None, :]
    owner_at = jnp.sum(jnp.where(slot_table, relay_owner[:, :, 0][:, :, None], 0), axis=1)
    moved = jnp.einsum(
        "sjcw,sjp->spcw", tiles, slot_table.astype(jnp.float32), precision=HIGH
    )

    def place(target):
        return jnp.where((owner_at == target)[:, :, None, None], moved, 0.0)

    from_below = shifted(place(2), "axial", 1)
    from_above = shifted(place(0), "axial", -1)
    received = (place(1) + from_below + from_above).reshape(
        STEPS, local_count, axial_cells, 2, band_width
    )
    loads = jnp.einsum("aqr,sazcr->sazcq", tile_weight, received, precision=HIGH).reshape(
        STEPS, local_count, axial_cells, 2 * band_width
    )
    for step_index in range(STEPS):
        velocity, strain, plastic = plastic_update(loads[step_index], velocity, strain, plastic)
    return (field_out, velocity, strain, plastic)


def solution(mesh):
    placed = (
        P("azim", "axial", None),
        P("azim", "axial", None),
        P(),
        P("azim", "axial", None),
        P("azim", None, None),
        P(None, "azim", "axial"),
        P(None, "azim", "axial"),
        P("azim", "axial", None),
        P("azim", "axial", None),
        P("azim", "axial", None),
    )
    return jax.shard_map(
        shards,
        mesh=mesh,
        in_specs=placed,
        out_specs=(
            P("azim", "axial", None),
            P("azim", "axial", None),
            P("azim", "axial", None),
            P("azim", "axial", None),
        ),
        check_vma=False,
    )
```

```python
import math

import jax
import numpy as np
import jax.numpy as jnp
from jax import lax
from jax.sharding import PartitionSpec as P

STEPS = 2
SWEEPS = 3


HIGH = lax.Precision.HIGHEST
KAPPA = 2.0
AIR_TERM = 0.05
R_CORE = 16.0
MU_COIL = 1.0
FORCE_K = 1.0
E_MOD = 1.0
YIELD_ZERO = 0.5
HARDEN = 0.3
TIME_STEP = 0.5
STIFFNESS = 0.5
DAMPING = 0.9


def with_halo(block, sides, width):
    for axis, dim in sides:
        count = lax.axis_size(axis)
        forward = [(i, i + 1) for i in range(count - 1)]
        backward = [(target, source) for source, target in forward]
        low = lax.ppermute(
            lax.slice_in_dim(block, block.shape[dim] - width, None, axis=dim), axis, forward
        )
        high = lax.ppermute(lax.slice_in_dim(block, 0, width, axis=dim), axis, backward)
        block = jnp.concatenate([low, block, high], axis=dim)
    return block


def shifted(array, axis, by):
    devices = lax.axis_size(axis)
    pairs = [(i, i + by) for i in range(devices) if 0 <= i + by < devices]
    return lax.ppermute(array, axis, pairs)


def harmonic_table(azimuth, harmonic, count_all):
    half_count = count_all // 2
    orders = jnp.where(harmonic <= half_count, harmonic, harmonic - half_count)
    phases = azimuth[:, None] * orders[None, :] % count_all
    angles = phases.astype(jnp.float32) * (2.0 * math.pi / count_all)
    return jnp.where(harmonic[None, :] <= half_count, jnp.cos(angles), jnp.sin(angles))


def harmonic_weight(harmonic, count_all):
    half_count = count_all // 2
    edge_mode = (harmonic == 0) | (harmonic == half_count)
    return jnp.where(edge_mode, 1.0 / count_all, 2.0 / count_all).astype(jnp.float32)


def harmonic_order(harmonic, count_all):
    half_count = count_all // 2
    return jnp.where(harmonic <= half_count, harmonic, harmonic - half_count).astype(jnp.float32)


def radial_profiles(radial_count, band_start, band_width):
    cell_index = jnp.arange(radial_count, dtype=jnp.int32)
    radius = R_CORE + cell_index.astype(jnp.float32)
    inside = (cell_index >= band_start) & (cell_index < band_start + band_width)
    conduct = jnp.where(inside, KAPPA, AIR_TERM).astype(jnp.float32)
    coil_zone = (cell_index < band_start).astype(jnp.float32)
    return (radius, conduct, coil_zone)


def radial_sum(iterate):
    radial_pad = jnp.pad(iterate, ((0, 0), (0, 0), (1, 1)))
    return radial_pad[:, :, 2:] + radial_pad[:, :, :-2]


def lorentz(padded, previous, conduct, radius, band_start, band_width):
    current_field = padded[:, 1:-1]
    axial_slope = (padded[:, 2:] - padded[:, :-2]) * 0.5
    radial_pad = jnp.pad(current_field, ((0, 0), (0, 0), (1, 1)))
    radial_slope = (radial_pad[:, :, 2:] - radial_pad[:, :, :-2]) * 0.5
    b_axial = radial_slope + current_field / radius
    eddy_current = -conduct * (current_field - previous)
    force_radial = FORCE_K * eddy_current * b_axial
    force_axial = FORCE_K * eddy_current * axial_slope
    return jnp.concatenate(
        [
            force_radial[..., band_start : band_start + band_width],
            force_axial[..., band_start : band_start + band_width],
        ],
        axis=-1,
    )


def plastic_update(load, velocity, strain, plastic):
    trial_stress = E_MOD * (strain - plastic)
    excess = jnp.abs(trial_stress) - YIELD_ZERO
    increment = (
        trial_stress
        * jnp.maximum(excess, 0.0)
        / ((E_MOD + HARDEN) * jnp.maximum(jnp.abs(trial_stress), YIELD_ZERO))
    )
    plastic = plastic + increment
    stress = E_MOD * (strain - plastic)
    velocity = DAMPING * velocity + TIME_STEP * (load - STIFFNESS * stress)
    strain = strain + TIME_STEP * velocity
    return (velocity, strain, plastic)


def basis_constant(count_all):
    half_count = count_all // 2
    harmonic = np.arange(count_all)
    orders = np.where(harmonic <= half_count, harmonic, harmonic - half_count)
    phases = (harmonic[:, None] * orders[None, :]) % count_all
    angles = phases.astype(np.float64) * (2.0 * math.pi / count_all)
    table = np.where(harmonic[None, :] <= half_count, np.cos(angles), np.sin(angles))
    return table.astype(np.float32)


def transform(flat, basis, inverse):
    rows, count = flat.shape
    devices = lax.axis_size("azim")
    unit = devices * 128 // math.gcd(rows, 128)
    padded = -(-count // unit) * unit
    flat = jnp.pad(flat, ((0, 0), (0, padded - count)))
    width = padded // devices
    dense = (devices, rows * width // 128, 128)
    blocks = flat.reshape(rows, devices, width).transpose(1, 0, 2).reshape(dense)
    spread = lax.all_to_all(blocks, "azim", 0, 0, tiled=True).reshape(devices * rows, width)
    contract = 1 if inverse else 0
    mixed = lax.dot_general(
        basis, spread, (((contract,), (0,)), ((), ())), precision=lax.Precision.HIGH,
        preferred_element_type=jnp.float32,
    )
    joined = lax.all_to_all(mixed.reshape(dense), "azim", 0, 0, tiled=True)
    return joined.reshape(devices, rows, width).transpose(1, 0, 2).reshape(rows, padded)[:, :count]


def lorentz_window(padded, previous, conduct, radius):
    current_field = padded[:, 1:-1]
    axial_slope = (padded[:, 2:] - padded[:, :-2]) * 0.5
    radial_pad = jnp.pad(current_field, ((0, 0), (0, 0), (1, 1)))
    radial_slope = (radial_pad[:, :, 2:] - radial_pad[:, :, :-2]) * 0.5
    b_axial = radial_slope + current_field / radius
    eddy_current = -conduct * (current_field - previous)
    force_radial = FORCE_K * eddy_current * b_axial
    force_axial = FORCE_K * eddy_current * axial_slope
    return jnp.concatenate([force_radial[..., 1:-1], force_axial[..., 1:-1]], axis=-1)


def shards(
    coil_density,
    coil_mask,
    drive,
    potential,
    tile_weight,
    relay_owner,
    relay_slot,
    velocity,
    strain,
    plastic,
):
    local_count, axial_cells, radial_cells = potential.shape
    band_width = tile_weight.shape[1]
    azim_total = local_count * lax.axis_size("azim")
    own_index = lax.axis_index("azim") * local_count + jnp.arange(local_count, dtype=jnp.int32)
    band_start = radial_cells // 4
    radius, conduct, coil_zone = radial_profiles(radial_cells, band_start, band_width)
    orders = harmonic_order(own_index, azim_total)
    diagonal_term = (
        4.0 + conduct[None, None, :] + (orders[:, None, None] / radius[None, None, :]) ** 2
    )
    basis = jnp.asarray(basis_constant(azim_total))

    coil = coil_density[..., :band_start] * coil_mask[..., :band_start].astype(jnp.float32)
    flat = jnp.concatenate(
        [potential.reshape(local_count, -1), coil.reshape(local_count, -1)], axis=1
    )
    modes = transform(flat, basis, inverse=False)
    split_at = axial_cells * radial_cells
    modes = jnp.concatenate(
        [
            modes[:, :split_at].reshape(local_count, axial_cells, radial_cells),
            modes[:, split_at:].reshape(local_count, axial_cells, band_start),
        ],
        axis=-1,
    )

    reach = STEPS * SWEEPS + 1
    modes = with_halo(modes, (("axial", 1),), reach)
    field_modes = modes[..., :radial_cells]
    coil_modes = jnp.pad(modes[..., radial_cells:], ((0, 0), (0, 0), (0, radial_cells - band_start)))
    span = axial_cells + 2 * reach
    global_z = lax.axis_index("axial") * axial_cells - reach + jnp.arange(span, dtype=jnp.int32)
    inside = ((global_z >= 0) & (global_z < axial_cells * lax.axis_size("axial")))[None, :, None]

    weight = harmonic_weight(own_index, azim_total)[:, None, None]
    window = slice(band_start - 1, band_start + band_width + 1)
    iterate = field_modes
    kept = []
    for step_index in range(STEPS):
        right_side = MU_COIL * (drive[step_index] * coil_modes) + conduct * iterate
        for sweep_index in range(SWEEPS):
            axial_pad = jnp.pad(iterate, ((0, 0), (1, 1), (0, 0)))
            nearby = axial_pad[:, 2:] + axial_pad[:, :-2] + radial_sum(iterate)
            iterate = jnp.where(inside, (right_side + nearby) / diagonal_term, 0.0)
        planes = iterate[:, reach - 1 : reach + axial_cells + 1] * weight
        kept.append(planes if step_index == STEPS - 1 else planes[..., window])
    pieces = [piece.shape for piece in kept]
    flat = transform(
        jnp.concatenate([piece.reshape(local_count, -1) for piece in kept], axis=1),
        basis,
        inverse=True,
    )
    fields, offset = [], 0
    for shape in pieces:
        size = math.prod(shape[1:])
        fields.append(flat[:, offset : offset + size].reshape(shape))
        offset += size

    previous = potential[..., window]
    tiles = []
    for step_index in range(STEPS):
        padded = fields[step_index]
        if step_index == STEPS - 1:
            field_out = padded[:, 1:-1]
            padded = padded[..., window]
        tiles.append(lorentz_window(padded, previous, conduct[window], radius[window]))
        previous = padded[:, 1:-1]
    tiles = jnp.stack(tiles)

    slot_range = jnp.arange(local_count, dtype=jnp.int32)
    slot_table = relay_slot[:, :, 0][:, :, None] == slot_range[None, None, :]
    owner_at = jnp.sum(jnp.where(slot_table, relay_owner[:, :, 0][:, :, None], 0), axis=1)
    moved = jnp.einsum(
        "sjcw,sjp->spcw", tiles, slot_table.astype(jnp.float32), precision=HIGH
    )

    def place(target):
        return jnp.where((owner_at == target)[:, :, None, None], moved, 0.0)

    from_below = shifted(place(2), "axial", 1)
    from_above = shifted(place(0), "axial", -1)
    received = (place(1) + from_below + from_above).reshape(
        STEPS, local_count, axial_cells, 2, band_width
    )
    loads = jnp.einsum(
        "aqr,sazcr->sazcq", tile_weight, received, precision=lax.Precision.HIGH
    ).reshape(
        STEPS, local_count, axial_cells, 2 * band_width
    )
    for step_index in range(STEPS):
        velocity, strain, plastic = plastic_update(loads[step_index], velocity, strain, plastic)
    return (field_out, velocity, strain, plastic)


def solution(mesh):
    placed = (
        P("azim", "axial", None),
        P("azim", "axial", None),
        P(),
        P("azim", "axial", None),
        P("azim", None, None),
        P(None, "azim", "axial"),
        P(None, "azim", "axial"),
        P("azim", "axial", None),
        P("azim", "axial", None),
        P("azim", "axial", None),
    )
    return jax.shard_map(
        shards,
        mesh=mesh,
        in_specs=placed,
        out_specs=(
            P("azim", "axial", None),
            P("azim", "axial", None),
            P("azim", "axial", None),
            P("azim", "axial", None),
        ),
        check_vma=False,
    )
```

```python
import math

import jax
import numpy as np
import jax.numpy as jnp
from jax import lax
from jax.sharding import PartitionSpec as P

STEPS = 2
SWEEPS = 3


HIGH = lax.Precision.HIGHEST
KAPPA = 2.0
AIR_TERM = 0.05
R_CORE = 16.0
MU_COIL = 1.0
FORCE_K = 1.0
E_MOD = 1.0
YIELD_ZERO = 0.5
HARDEN = 0.3
TIME_STEP = 0.5
STIFFNESS = 0.5
DAMPING = 0.9


def with_halo(block, sides, width):
    for axis, dim in sides:
        count = lax.axis_size(axis)
        forward = [(i, i + 1) for i in range(count - 1)]
        backward = [(target, source) for source, target in forward]
        low = lax.ppermute(
            lax.slice_in_dim(block, block.shape[dim] - width, None, axis=dim), axis, forward
        )
        high = lax.ppermute(lax.slice_in_dim(block, 0, width, axis=dim), axis, backward)
        block = jnp.concatenate([low, block, high], axis=dim)
    return block


def shifted(array, axis, by):
    devices = lax.axis_size(axis)
    pairs = [(i, i + by) for i in range(devices) if 0 <= i + by < devices]
    return lax.ppermute(array, axis, pairs)


def harmonic_table(azimuth, harmonic, count_all):
    half_count = count_all // 2
    orders = jnp.where(harmonic <= half_count, harmonic, harmonic - half_count)
    phases = azimuth[:, None] * orders[None, :] % count_all
    angles = phases.astype(jnp.float32) * (2.0 * math.pi / count_all)
    return jnp.where(harmonic[None, :] <= half_count, jnp.cos(angles), jnp.sin(angles))


def harmonic_weight(harmonic, count_all):
    half_count = count_all // 2
    edge_mode = (harmonic == 0) | (harmonic == half_count)
    return jnp.where(edge_mode, 1.0 / count_all, 2.0 / count_all).astype(jnp.float32)


def harmonic_order(harmonic, count_all):
    half_count = count_all // 2
    return jnp.where(harmonic <= half_count, harmonic, harmonic - half_count).astype(jnp.float32)


def radial_profiles(radial_count, band_start, band_width):
    cell_index = jnp.arange(radial_count, dtype=jnp.int32)
    radius = R_CORE + cell_index.astype(jnp.float32)
    inside = (cell_index >= band_start) & (cell_index < band_start + band_width)
    conduct = jnp.where(inside, KAPPA, AIR_TERM).astype(jnp.float32)
    coil_zone = (cell_index < band_start).astype(jnp.float32)
    return (radius, conduct, coil_zone)


def radial_sum(iterate):
    radial_pad = jnp.pad(iterate, ((0, 0), (0, 0), (1, 1)))
    return radial_pad[:, :, 2:] + radial_pad[:, :, :-2]


def lorentz(padded, previous, conduct, radius, band_start, band_width):
    current_field = padded[:, 1:-1]
    axial_slope = (padded[:, 2:] - padded[:, :-2]) * 0.5
    radial_pad = jnp.pad(current_field, ((0, 0), (0, 0), (1, 1)))
    radial_slope = (radial_pad[:, :, 2:] - radial_pad[:, :, :-2]) * 0.5
    b_axial = radial_slope + current_field / radius
    eddy_current = -conduct * (current_field - previous)
    force_radial = FORCE_K * eddy_current * b_axial
    force_axial = FORCE_K * eddy_current * axial_slope
    return jnp.concatenate(
        [
            force_radial[..., band_start : band_start + band_width],
            force_axial[..., band_start : band_start + band_width],
        ],
        axis=-1,
    )


def plastic_update(load, velocity, strain, plastic):
    trial_stress = E_MOD * (strain - plastic)
    excess = jnp.abs(trial_stress) - YIELD_ZERO
    increment = (
        trial_stress
        * jnp.maximum(excess, 0.0)
        / ((E_MOD + HARDEN) * jnp.maximum(jnp.abs(trial_stress), YIELD_ZERO))
    )
    plastic = plastic + increment
    stress = E_MOD * (strain - plastic)
    velocity = DAMPING * velocity + TIME_STEP * (load - STIFFNESS * stress)
    strain = strain + TIME_STEP * velocity
    return (velocity, strain, plastic)


def basis_constant(count_all):
    half_count = count_all // 2
    harmonic = np.arange(count_all)
    orders = np.where(harmonic <= half_count, harmonic, harmonic - half_count)
    phases = (harmonic[:, None] * orders[None, :]) % count_all
    angles = phases.astype(np.float64) * (2.0 * math.pi / count_all)
    table = np.where(harmonic[None, :] <= half_count, np.cos(angles), np.sin(angles))
    return table.astype(np.float32)


def transform(flat, basis, inverse):
    rows, count = flat.shape
    devices = lax.axis_size("azim")
    unit = devices * 128 // math.gcd(rows, 128)
    padded = -(-count // unit) * unit
    flat = jnp.pad(flat, ((0, 0), (0, padded - count)))
    width = padded // devices
    dense = (devices, rows * width // 128, 128)
    blocks = flat.reshape(rows, devices, width).transpose(1, 0, 2).reshape(dense)
    spread = lax.all_to_all(blocks, "azim", 0, 0, tiled=True).reshape(devices * rows, width)
    contract = 1 if inverse else 0
    mixed = lax.dot_general(
        basis, spread, (((contract,), (0,)), ((), ())), precision=lax.Precision.HIGH,
        preferred_element_type=jnp.float32,
    )
    joined = lax.all_to_all(mixed.reshape(dense), "azim", 0, 0, tiled=True)
    return joined.reshape(devices, rows, width).transpose(1, 0, 2).reshape(rows, padded)[:, :count]


def lorentz_window(padded, previous, conduct, radius):
    current_field = padded[:, 1:-1]
    axial_slope = (padded[:, 2:] - padded[:, :-2]) * 0.5
    radial_pad = jnp.pad(current_field, ((0, 0), (0, 0), (1, 1)))
    radial_slope = (radial_pad[:, :, 2:] - radial_pad[:, :, :-2]) * 0.5
    b_axial = radial_slope + current_field / radius
    eddy_current = -conduct * (current_field - previous)
    force_radial = FORCE_K * eddy_current * b_axial
    force_axial = FORCE_K * eddy_current * axial_slope
    return jnp.concatenate([force_radial[..., 1:-1], force_axial[..., 1:-1]], axis=-1)


def shards(
    coil_density,
    coil_mask,
    drive,
    potential,
    tile_weight,
    relay_owner,
    relay_slot,
    velocity,
    strain,
    plastic,
):
    local_count, axial_cells, radial_cells = potential.shape
    band_width = tile_weight.shape[1]
    azim_total = local_count * lax.axis_size("azim")
    own_index = lax.axis_index("azim") * local_count + jnp.arange(local_count, dtype=jnp.int32)
    band_start = radial_cells // 4
    radius, conduct, coil_zone = radial_profiles(radial_cells, band_start, band_width)
    orders = harmonic_order(own_index, azim_total)
    diagonal_term = (
        4.0 + conduct[None, None, :] + (orders[:, None, None] / radius[None, None, :]) ** 2
    )
    basis = jnp.asarray(basis_constant(azim_total))

    coil = coil_density[..., :band_start] * coil_mask[..., :band_start].astype(jnp.float32)
    flat = jnp.concatenate(
        [potential.reshape(local_count, -1), coil.reshape(local_count, -1)], axis=1
    )
    modes = transform(flat, basis, inverse=False)
    split_at = axial_cells * radial_cells
    modes = jnp.concatenate(
        [
            modes[:, :split_at].reshape(local_count, axial_cells, radial_cells),
            modes[:, split_at:].reshape(local_count, axial_cells, band_start),
        ],
        axis=-1,
    )

    reach = STEPS * SWEEPS + 1
    modes = with_halo(modes, (("axial", 1),), reach)
    field_modes = modes[..., :radial_cells]
    coil_modes = jnp.pad(modes[..., radial_cells:], ((0, 0), (0, 0), (0, radial_cells - band_start)))
    span = axial_cells + 2 * reach
    global_z = lax.axis_index("axial") * axial_cells - reach + jnp.arange(span, dtype=jnp.int32)
    inside = ((global_z >= 0) & (global_z < axial_cells * lax.axis_size("axial")))[None, :, None]
    divisor = jnp.where(inside, diagonal_term, jnp.inf)

    weight = harmonic_weight(own_index, azim_total)[:, None, None]
    window = slice(band_start - 1, band_start + band_width + 1)
    iterate = field_modes
    kept = []
    for step_index in range(STEPS):
        right_side = MU_COIL * (drive[step_index] * coil_modes) + conduct * iterate
        for sweep_index in range(SWEEPS):
            axial_pad = jnp.pad(iterate, ((0, 0), (1, 1), (0, 0)))
            nearby = axial_pad[:, 2:] + axial_pad[:, :-2] + radial_sum(iterate)
            iterate = (right_side + nearby) / divisor
        planes = iterate[:, reach - 1 : reach + axial_cells + 1] * weight
        kept.append(planes if step_index == STEPS - 1 else planes[..., window])
    pieces = [piece.shape for piece in kept]
    flat = transform(
        jnp.concatenate([piece.reshape(local_count, -1) for piece in kept], axis=1),
        basis,
        inverse=True,
    )
    fields, offset = [], 0
    for shape in pieces:
        size = math.prod(shape[1:])
        fields.append(flat[:, offset : offset + size].reshape(shape))
        offset += size

    previous = potential[..., window]
    tiles = []
    for step_index in range(STEPS):
        padded = fields[step_index]
        if step_index == STEPS - 1:
            field_out = padded[:, 1:-1]
            padded = padded[..., window]
        tiles.append(lorentz_window(padded, previous, conduct[window], radius[window]))
        previous = padded[:, 1:-1]
    tiles = jnp.stack(tiles)

    slot_range = jnp.arange(local_count, dtype=jnp.int32)
    slot_table = relay_slot[:, :, 0][:, :, None] == slot_range[None, None, :]
    owner_at = jnp.sum(jnp.where(slot_table, relay_owner[:, :, 0][:, :, None], 0), axis=1)
    moved = jnp.einsum(
        "sjcw,sjp->spcw", tiles, slot_table.astype(jnp.float32), precision=HIGH
    )

    def place(target):
        return jnp.where((owner_at == target)[:, :, None, None], moved, 0.0)

    from_below = shifted(place(2), "axial", 1)
    from_above = shifted(place(0), "axial", -1)
    received = place(1) + from_below + from_above
    blank = jnp.zeros_like(tile_weight)
    paired = jnp.concatenate(
        [
            jnp.concatenate([tile_weight, blank], axis=2),
            jnp.concatenate([blank, tile_weight], axis=2),
        ],
        axis=1,
    )
    loads = jnp.einsum("aqr,sazr->sazq", paired, received, precision=lax.Precision.HIGH)
    for step_index in range(STEPS):
        velocity, strain, plastic = plastic_update(loads[step_index], velocity, strain, plastic)
    return (field_out, velocity, strain, plastic)


def solution(mesh):
    placed = (
        P("azim", "axial", None),
        P("azim", "axial", None),
        P(),
        P("azim", "axial", None),
        P("azim", None, None),
        P(None, "azim", "axial"),
        P(None, "azim", "axial"),
        P("azim", "axial", None),
        P("azim", "axial", None),
        P("azim", "axial", None),
    )
    return jax.shard_map(
        shards,
        mesh=mesh,
        in_specs=placed,
        out_specs=(
            P("azim", "axial", None),
            P("azim", "axial", None),
            P("azim", "axial", None),
            P("azim", "axial", None),
        ),
        check_vma=False,
    )
```

```python
import math

import jax
import numpy as np
import jax.numpy as jnp
from jax import lax
from jax.sharding import PartitionSpec as P

STEPS = 2
SWEEPS = 3


HIGH = lax.Precision.HIGHEST
KAPPA = 2.0
AIR_TERM = 0.05
R_CORE = 16.0
MU_COIL = 1.0
FORCE_K = 1.0
E_MOD = 1.0
YIELD_ZERO = 0.5
HARDEN = 0.3
TIME_STEP = 0.5
STIFFNESS = 0.5
DAMPING = 0.9


def with_halo(block, sides, width):
    for axis, dim in sides:
        count = lax.axis_size(axis)
        forward = [(i, i + 1) for i in range(count - 1)]
        backward = [(target, source) for source, target in forward]
        low = lax.ppermute(
            lax.slice_in_dim(block, block.shape[dim] - width, None, axis=dim), axis, forward
        )
        high = lax.ppermute(lax.slice_in_dim(block, 0, width, axis=dim), axis, backward)
        block = jnp.concatenate([low, block, high], axis=dim)
    return block


def shifted(array, axis, by):
    devices = lax.axis_size(axis)
    pairs = [(i, i + by) for i in range(devices) if 0 <= i + by < devices]
    return lax.ppermute(array, axis, pairs)


def harmonic_table(azimuth, harmonic, count_all):
    half_count = count_all // 2
    orders = jnp.where(harmonic <= half_count, harmonic, harmonic - half_count)
    phases = azimuth[:, None] * orders[None, :] % count_all
    angles = phases.astype(jnp.float32) * (2.0 * math.pi / count_all)
    return jnp.where(harmonic[None, :] <= half_count, jnp.cos(angles), jnp.sin(angles))


def harmonic_weight(harmonic, count_all):
    half_count = count_all // 2
    edge_mode = (harmonic == 0) | (harmonic == half_count)
    return jnp.where(edge_mode, 1.0 / count_all, 2.0 / count_all).astype(jnp.float32)


def harmonic_order(harmonic, count_all):
    half_count = count_all // 2
    return jnp.where(harmonic <= half_count, harmonic, harmonic - half_count).astype(jnp.float32)


def radial_profiles(radial_count, band_start, band_width):
    cell_index = jnp.arange(radial_count, dtype=jnp.int32)
    radius = R_CORE + cell_index.astype(jnp.float32)
    inside = (cell_index >= band_start) & (cell_index < band_start + band_width)
    conduct = jnp.where(inside, KAPPA, AIR_TERM).astype(jnp.float32)
    coil_zone = (cell_index < band_start).astype(jnp.float32)
    return (radius, conduct, coil_zone)


def radial_sum(iterate):
    radial_pad = jnp.pad(iterate, ((0, 0), (0, 0), (1, 1)))
    return radial_pad[:, :, 2:] + radial_pad[:, :, :-2]


def lorentz(padded, previous, conduct, radius, band_start, band_width):
    current_field = padded[:, 1:-1]
    axial_slope = (padded[:, 2:] - padded[:, :-2]) * 0.5
    radial_pad = jnp.pad(current_field, ((0, 0), (0, 0), (1, 1)))
    radial_slope = (radial_pad[:, :, 2:] - radial_pad[:, :, :-2]) * 0.5
    b_axial = radial_slope + current_field / radius
    eddy_current = -conduct * (current_field - previous)
    force_radial = FORCE_K * eddy_current * b_axial
    force_axial = FORCE_K * eddy_current * axial_slope
    return jnp.concatenate(
        [
            force_radial[..., band_start : band_start + band_width],
            force_axial[..., band_start : band_start + band_width],
        ],
        axis=-1,
    )


def plastic_update(load, velocity, strain, plastic):
    trial_stress = E_MOD * (strain - plastic)
    excess = jnp.abs(trial_stress) - YIELD_ZERO
    increment = (
        trial_stress
        * jnp.maximum(excess, 0.0)
        / ((E_MOD + HARDEN) * jnp.maximum(jnp.abs(trial_stress), YIELD_ZERO))
    )
    plastic = plastic + increment
    stress = E_MOD * (strain - plastic)
    velocity = DAMPING * velocity + TIME_STEP * (load - STIFFNESS * stress)
    strain = strain + TIME_STEP * velocity
    return (velocity, strain, plastic)


def basis_constant(count_all):
    half_count = count_all // 2
    harmonic = np.arange(count_all)
    orders = np.where(harmonic <= half_count, harmonic, harmonic - half_count)
    phases = (harmonic[:, None] * orders[None, :]) % count_all
    angles = phases.astype(np.float64) * (2.0 * math.pi / count_all)
    table = np.where(harmonic[None, :] <= half_count, np.cos(angles), np.sin(angles))
    return table.astype(np.float32)


def transform(main, rest, basis, inverse):
    devices, rows, lanes = main.shape
    count = rest.shape[1]
    unit = devices * lanes // math.gcd(rows, lanes)
    padded = -(-count // unit) * unit
    width = padded // devices
    packed = (devices, rows * width // lanes, lanes)
    rest = jnp.pad(rest, ((0, 0), (0, padded - count)))
    rest = rest.reshape(rows, devices, width).transpose(1, 0, 2).reshape(packed)
    spread = lax.all_to_all(
        jnp.concatenate([main, rest], axis=1), "azim", 0, 0, tiled=True
    )
    contract = 1 if inverse else 0

    def mix(columns):
        return lax.dot_general(
            basis, columns, (((contract,), (0,)), ((), ())), precision=lax.Precision.HIGH,
            preferred_element_type=jnp.float32,
        )

    mixed_main = mix(spread[:, :rows].reshape(devices * rows, lanes)).reshape(main.shape)
    mixed_rest = mix(spread[:, rows:].reshape(devices * rows, width)).reshape(packed)
    joined = lax.all_to_all(
        jnp.concatenate([mixed_main, mixed_rest], axis=1), "azim", 0, 0, tiled=True
    )
    rest = joined[:, rows:].reshape(devices, rows, width).transpose(1, 0, 2)
    return joined[:, :rows], rest.reshape(rows, padded)[:, :count]


def lorentz_window(padded, previous, conduct, radius):
    current_field = padded[:, 1:-1]
    axial_slope = (padded[:, 2:] - padded[:, :-2]) * 0.5
    radial_pad = jnp.pad(current_field, ((0, 0), (0, 0), (1, 1)))
    radial_slope = (radial_pad[:, :, 2:] - radial_pad[:, :, :-2]) * 0.5
    b_axial = radial_slope + current_field / radius
    eddy_current = -conduct * (current_field - previous)
    force_radial = FORCE_K * eddy_current * b_axial
    force_axial = FORCE_K * eddy_current * axial_slope
    return jnp.concatenate([force_radial[..., 1:-1], force_axial[..., 1:-1]], axis=-1)


def shards(
    coil_density,
    coil_mask,
    drive,
    potential,
    tile_weight,
    relay_owner,
    relay_slot,
    velocity,
    strain,
    plastic,
):
    local_count, axial_cells, radial_cells = potential.shape
    band_width = tile_weight.shape[1]
    azim_total = local_count * lax.axis_size("azim")
    own_index = lax.axis_index("azim") * local_count + jnp.arange(local_count, dtype=jnp.int32)
    band_start = radial_cells // 4
    radius, conduct, coil_zone = radial_profiles(radial_cells, band_start, band_width)
    orders = harmonic_order(own_index, azim_total)
    diagonal_term = (
        4.0 + conduct[None, None, :] + (orders[:, None, None] / radius[None, None, :]) ** 2
    )
    basis = jnp.asarray(basis_constant(azim_total))

    coil = coil_density[..., :band_start] * coil_mask[..., :band_start].astype(jnp.float32)
    field_modes, coil_modes = transform(
        potential.transpose(1, 0, 2), coil.reshape(local_count, -1), basis, inverse=False
    )
    modes = jnp.concatenate(
        [
            field_modes.transpose(1, 0, 2),
            coil_modes.reshape(local_count, axial_cells, band_start),
        ],
        axis=-1,
    )

    reach = STEPS * SWEEPS + 1
    modes = with_halo(modes, (("axial", 1),), reach)
    field_modes = modes[..., :radial_cells]
    coil_modes = jnp.pad(modes[..., radial_cells:], ((0, 0), (0, 0), (0, radial_cells - band_start)))
    span = axial_cells + 2 * reach
    global_z = lax.axis_index("axial") * axial_cells - reach + jnp.arange(span, dtype=jnp.int32)
    inside = ((global_z >= 0) & (global_z < axial_cells * lax.axis_size("axial")))[None, :, None]
    divisor = jnp.where(inside, diagonal_term, jnp.inf)

    weight = harmonic_weight(own_index, azim_total)[:, None, None]
    window = slice(band_start - 1, band_start + band_width + 1)
    iterate = field_modes
    kept = []
    for step_index in range(STEPS):
        right_side = MU_COIL * (drive[step_index] * coil_modes) + conduct * iterate
        for sweep_index in range(SWEEPS):
            axial_pad = jnp.pad(iterate, ((0, 0), (1, 1), (0, 0)))
            nearby = axial_pad[:, 2:] + axial_pad[:, :-2] + radial_sum(iterate)
            iterate = (right_side + nearby) / divisor
        kept.append(iterate[:, reach - 1 : reach + axial_cells + 1] * weight)
    last = kept[-1]
    edges = jnp.concatenate([last[:, :1], last[:, -1:]], axis=1)[..., window]
    pieces = [edges.shape] + [piece[..., window].shape for piece in kept[:-1]]
    extra = jnp.concatenate(
        [edges.reshape(local_count, -1)]
        + [piece[..., window].reshape(local_count, -1) for piece in kept[:-1]],
        axis=1,
    )
    planes, extra = transform(last[:, 1:-1].transpose(1, 0, 2), extra, basis, inverse=True)
    field_out = planes.transpose(1, 0, 2)
    unpacked, offset = [], 0
    for shape in pieces:
        size = math.prod(shape[1:])
        unpacked.append(extra[:, offset : offset + size].reshape(shape))
        offset += size
    edges = unpacked[0]
    fields = unpacked[1:] + [
        jnp.concatenate([edges[:, :1], field_out[..., window], edges[:, 1:]], axis=1)
    ]

    previous = potential[..., window]
    tiles = []
    for step_index in range(STEPS):
        padded = fields[step_index]
        tiles.append(lorentz_window(padded, previous, conduct[window], radius[window]))
        previous = padded[:, 1:-1]
    tiles = jnp.stack(tiles)

    slot_range = jnp.arange(local_count, dtype=jnp.int32)
    slot_table = relay_slot[:, :, 0][:, :, None] == slot_range[None, None, :]
    owner_at = jnp.sum(jnp.where(slot_table, relay_owner[:, :, 0][:, :, None], 0), axis=1)
    moved = jnp.einsum(
        "sjcw,sjp->spcw", tiles, slot_table.astype(jnp.float32), precision=HIGH
    )

    def place(target):
        return jnp.where((owner_at == target)[:, :, None, None], moved, 0.0)

    from_below = shifted(place(2), "axial", 1)
    from_above = shifted(place(0), "axial", -1)
    received = place(1) + from_below + from_above
    blank = jnp.zeros_like(tile_weight)
    paired = jnp.concatenate(
        [
            jnp.concatenate([tile_weight, blank], axis=2),
            jnp.concatenate([blank, tile_weight], axis=2),
        ],
        axis=1,
    )
    loads = jnp.einsum("aqr,sazr->sazq", paired, received, precision=lax.Precision.HIGH)
    for step_index in range(STEPS):
        velocity, strain, plastic = plastic_update(loads[step_index], velocity, strain, plastic)
    return (field_out, velocity, strain, plastic)


def solution(mesh):
    placed = (
        P("azim", "axial", None),
        P("azim", "axial", None),
        P(),
        P("azim", "axial", None),
        P("azim", None, None),
        P(None, "azim", "axial"),
        P(None, "azim", "axial"),
        P("azim", "axial", None),
        P("azim", "axial", None),
        P("azim", "axial", None),
    )
    return jax.shard_map(
        shards,
        mesh=mesh,
        in_specs=placed,
        out_specs=(
            P("azim", "axial", None),
            P("azim", "axial", None),
            P("azim", "axial", None),
            P("azim", "axial", None),
        ),
        check_vma=False,
    )
```

```python
import math

import jax
import numpy as np
import jax.numpy as jnp
from jax import lax
from jax.sharding import PartitionSpec as P

STEPS = 2
SWEEPS = 3


HIGH = lax.Precision.HIGHEST
KAPPA = 2.0
AIR_TERM = 0.05
R_CORE = 16.0
MU_COIL = 1.0
FORCE_K = 1.0
E_MOD = 1.0
YIELD_ZERO = 0.5
HARDEN = 0.3
TIME_STEP = 0.5
STIFFNESS = 0.5
DAMPING = 0.9


def with_halo(block, sides, width):
    for axis, dim in sides:
        count = lax.axis_size(axis)
        forward = [(i, i + 1) for i in range(count - 1)]
        backward = [(target, source) for source, target in forward]
        low = lax.ppermute(
            lax.slice_in_dim(block, block.shape[dim] - width, None, axis=dim), axis, forward
        )
        high = lax.ppermute(lax.slice_in_dim(block, 0, width, axis=dim), axis, backward)
        block = jnp.concatenate([low, block, high], axis=dim)
    return block


def shifted(array, axis, by):
    devices = lax.axis_size(axis)
    pairs = [(i, i + by) for i in range(devices) if 0 <= i + by < devices]
    return lax.ppermute(array, axis, pairs)


def harmonic_table(azimuth, harmonic, count_all):
    half_count = count_all // 2
    orders = jnp.where(harmonic <= half_count, harmonic, harmonic - half_count)
    phases = azimuth[:, None] * orders[None, :] % count_all
    angles = phases.astype(jnp.float32) * (2.0 * math.pi / count_all)
    return jnp.where(harmonic[None, :] <= half_count, jnp.cos(angles), jnp.sin(angles))


def harmonic_weight(harmonic, count_all):
    half_count = count_all // 2
    edge_mode = (harmonic == 0) | (harmonic == half_count)
    return jnp.where(edge_mode, 1.0 / count_all, 2.0 / count_all).astype(jnp.float32)


def harmonic_order(harmonic, count_all):
    half_count = count_all // 2
    return jnp.where(harmonic <= half_count, harmonic, harmonic - half_count).astype(jnp.float32)


def radial_profiles(radial_count, band_start, band_width):
    cell_index = jnp.arange(radial_count, dtype=jnp.int32)
    radius = R_CORE + cell_index.astype(jnp.float32)
    inside = (cell_index >= band_start) & (cell_index < band_start + band_width)
    conduct = jnp.where(inside, KAPPA, AIR_TERM).astype(jnp.float32)
    coil_zone = (cell_index < band_start).astype(jnp.float32)
    return (radius, conduct, coil_zone)


def radial_sum(iterate):
    radial_pad = jnp.pad(iterate, ((0, 0), (0, 0), (1, 1)))
    return radial_pad[:, :, 2:] + radial_pad[:, :, :-2]


def lorentz(padded, previous, conduct, radius, band_start, band_width):
    current_field = padded[:, 1:-1]
    axial_slope = (padded[:, 2:] - padded[:, :-2]) * 0.5
    radial_pad = jnp.pad(current_field, ((0, 0), (0, 0), (1, 1)))
    radial_slope = (radial_pad[:, :, 2:] - radial_pad[:, :, :-2]) * 0.5
    b_axial = radial_slope + current_field / radius
    eddy_current = -conduct * (current_field - previous)
    force_radial = FORCE_K * eddy_current * b_axial
    force_axial = FORCE_K * eddy_current * axial_slope
    return jnp.concatenate(
        [
            force_radial[..., band_start : band_start + band_width],
            force_axial[..., band_start : band_start + band_width],
        ],
        axis=-1,
    )


def plastic_update(load, velocity, strain, plastic):
    trial_stress = E_MOD * (strain - plastic)
    excess = jnp.abs(trial_stress) - YIELD_ZERO
    increment = (
        trial_stress
        * jnp.maximum(excess, 0.0)
        / ((E_MOD + HARDEN) * jnp.maximum(jnp.abs(trial_stress), YIELD_ZERO))
    )
    plastic = plastic + increment
    stress = E_MOD * (strain - plastic)
    velocity = DAMPING * velocity + TIME_STEP * (load - STIFFNESS * stress)
    strain = strain + TIME_STEP * velocity
    return (velocity, strain, plastic)


def basis_constant(count_all):
    half_count = count_all // 2
    harmonic = np.arange(count_all)
    orders = np.where(harmonic <= half_count, harmonic, harmonic - half_count)
    phases = (harmonic[:, None] * orders[None, :]) % count_all
    angles = phases.astype(np.float64) * (2.0 * math.pi / count_all)
    table = np.where(harmonic[None, :] <= half_count, np.cos(angles), np.sin(angles))
    return table.astype(np.float32)


def transform(main, rest, basis, inverse):
    devices, rows, lanes = main.shape
    count = rest.shape[1]
    unit = devices * lanes // math.gcd(rows, lanes)
    padded = -(-count // unit) * unit
    width = padded // devices
    packed = (devices, rows * width // lanes, lanes)
    rest = jnp.pad(rest, ((0, 0), (0, padded - count)))
    rest = rest.reshape(rows, devices, width).transpose(1, 0, 2).reshape(packed)
    spread = lax.all_to_all(
        jnp.concatenate([main, rest], axis=1), "azim", 0, 0, tiled=True
    )
    contract = 1 if inverse else 0

    def mix(columns):
        return lax.dot_general(
            basis, columns, (((contract,), (0,)), ((), ())), precision=lax.Precision.HIGH,
            preferred_element_type=jnp.float32,
        )

    mixed = mix(
        jnp.concatenate(
            [
                spread[:, :rows].reshape(devices * rows, lanes),
                spread[:, rows:].reshape(devices * rows, width),
            ],
            axis=1,
        )
    )
    mixed_main = mixed[:, :lanes].reshape(main.shape)
    mixed_rest = mixed[:, lanes:].reshape(packed)
    joined = lax.all_to_all(
        jnp.concatenate([mixed_main, mixed_rest], axis=1), "azim", 0, 0, tiled=True
    )
    rest = joined[:, rows:].reshape(devices, rows, width).transpose(1, 0, 2)
    return joined[:, :rows], rest.reshape(rows, padded)[:, :count]


def lorentz_window(padded, previous, conduct, radius):
    current_field = padded[:, 1:-1]
    axial_slope = (padded[:, 2:] - padded[:, :-2]) * 0.5
    radial_pad = jnp.pad(current_field, ((0, 0), (0, 0), (1, 1)))
    radial_slope = (radial_pad[:, :, 2:] - radial_pad[:, :, :-2]) * 0.5
    b_axial = radial_slope + current_field / radius
    eddy_current = -conduct * (current_field - previous)
    force_radial = FORCE_K * eddy_current * b_axial
    force_axial = FORCE_K * eddy_current * axial_slope
    return jnp.concatenate([force_radial[..., 1:-1], force_axial[..., 1:-1]], axis=-1)


def shards(
    coil_density,
    coil_mask,
    drive,
    potential,
    tile_weight,
    relay_owner,
    relay_slot,
    velocity,
    strain,
    plastic,
):
    local_count, axial_cells, radial_cells = potential.shape
    band_width = tile_weight.shape[1]
    azim_total = local_count * lax.axis_size("azim")
    own_index = lax.axis_index("azim") * local_count + jnp.arange(local_count, dtype=jnp.int32)
    band_start = radial_cells // 4
    radius, conduct, coil_zone = radial_profiles(radial_cells, band_start, band_width)
    orders = harmonic_order(own_index, azim_total)
    diagonal_term = (
        4.0 + conduct[None, None, :] + (orders[:, None, None] / radius[None, None, :]) ** 2
    )
    basis = jnp.asarray(basis_constant(azim_total))

    coil = coil_density[..., :band_start] * coil_mask[..., :band_start].astype(jnp.float32)
    field_modes, coil_modes = transform(
        potential.transpose(1, 0, 2), coil.reshape(local_count, -1), basis, inverse=False
    )
    modes = jnp.concatenate(
        [
            field_modes.transpose(1, 0, 2),
            coil_modes.reshape(local_count, axial_cells, band_start),
        ],
        axis=-1,
    )

    reach = STEPS * SWEEPS + 1
    modes = with_halo(modes, (("axial", 1),), reach)
    field_modes = modes[..., :radial_cells]
    coil_modes = jnp.pad(modes[..., radial_cells:], ((0, 0), (0, 0), (0, radial_cells - band_start)))
    span = axial_cells + 2 * reach
    global_z = lax.axis_index("axial") * axial_cells - reach + jnp.arange(span, dtype=jnp.int32)
    inside = ((global_z >= 0) & (global_z < axial_cells * lax.axis_size("axial")))[None, :, None]
    divisor = jnp.where(inside, diagonal_term, jnp.inf)

    weight = harmonic_weight(own_index, azim_total)[:, None, None]
    window = slice(band_start - 1, band_start + band_width + 1)
    iterate = field_modes
    kept = []
    for step_index in range(STEPS):
        right_side = MU_COIL * (drive[step_index] * coil_modes) + conduct * iterate
        for sweep_index in range(SWEEPS):
            axial_pad = jnp.pad(iterate, ((0, 0), (1, 1), (0, 0)))
            nearby = axial_pad[:, 2:] + axial_pad[:, :-2] + radial_sum(iterate)
            iterate = (right_side + nearby) / divisor
        kept.append(iterate[:, reach - 1 : reach + axial_cells + 1] * weight)
    last = kept[-1]
    edges = jnp.concatenate([last[:, :1], last[:, -1:]], axis=1)[..., window]
    pieces = [edges.shape] + [piece[..., window].shape for piece in kept[:-1]]
    extra = jnp.concatenate(
        [edges.reshape(local_count, -1)]
        + [piece[..., window].reshape(local_count, -1) for piece in kept[:-1]],
        axis=1,
    )
    planes, extra = transform(last[:, 1:-1].transpose(1, 0, 2), extra, basis, inverse=True)
    field_out = planes.transpose(1, 0, 2)
    unpacked, offset = [], 0
    for shape in pieces:
        size = math.prod(shape[1:])
        unpacked.append(extra[:, offset : offset + size].reshape(shape))
        offset += size
    edges = unpacked[0]
    fields = unpacked[1:] + [
        jnp.concatenate([edges[:, :1], field_out[..., window], edges[:, 1:]], axis=1)
    ]

    previous = potential[..., window]
    tiles = []
    for step_index in range(STEPS):
        padded = fields[step_index]
        tiles.append(lorentz_window(padded, previous, conduct[window], radius[window]))
        previous = padded[:, 1:-1]
    tiles = jnp.stack(tiles)

    slot_range = jnp.arange(local_count, dtype=jnp.int32)
    slot_table = relay_slot[:, :, 0][:, :, None] == slot_range[None, None, :]
    owner_at = jnp.sum(jnp.where(slot_table, relay_owner[:, :, 0][:, :, None], 0), axis=1)
    moved = jnp.einsum(
        "sjcw,sjp->spcw", tiles, slot_table.astype(jnp.float32), precision=HIGH
    )

    blank = jnp.zeros_like(tile_weight)
    paired = jnp.concatenate(
        [
            jnp.concatenate([tile_weight, blank], axis=2),
            jnp.concatenate([blank, tile_weight], axis=2),
        ],
        axis=1,
    )
    mapped = jnp.einsum("apr,sazr->sazp", paired, moved, precision=lax.Precision.HIGH)

    def place(target):
        return jnp.where((owner_at == target)[:, :, None, None], mapped, 0.0)

    from_below = shifted(place(2), "axial", 1)
    from_above = shifted(place(0), "axial", -1)
    loads = place(1) + from_below + from_above
    for step_index in range(STEPS):
        velocity, strain, plastic = plastic_update(loads[step_index], velocity, strain, plastic)
    return (field_out, velocity, strain, plastic)


def solution(mesh):
    placed = (
        P("azim", "axial", None),
        P("azim", "axial", None),
        P(),
        P("azim", "axial", None),
        P("azim", None, None),
        P(None, "azim", "axial"),
        P(None, "azim", "axial"),
        P("azim", "axial", None),
        P("azim", "axial", None),
        P("azim", "axial", None),
    )
    return jax.shard_map(
        shards,
        mesh=mesh,
        in_specs=placed,
        out_specs=(
            P("azim", "axial", None),
            P("azim", "axial", None),
            P("azim", "axial", None),
            P("azim", "axial", None),
        ),
        check_vma=False,
    )
```

```python
import math

import jax
import numpy as np
import jax.numpy as jnp
from jax import lax
from jax.sharding import PartitionSpec as P

STEPS = 2
SWEEPS = 3


HIGH = lax.Precision.HIGHEST
KAPPA = 2.0
AIR_TERM = 0.05
R_CORE = 16.0
MU_COIL = 1.0
FORCE_K = 1.0
E_MOD = 1.0
YIELD_ZERO = 0.5
HARDEN = 0.3
TIME_STEP = 0.5
STIFFNESS = 0.5
DAMPING = 0.9


def with_halo(block, sides, width):
    for axis, dim in sides:
        count = lax.axis_size(axis)
        forward = [(i, i + 1) for i in range(count - 1)]
        backward = [(target, source) for source, target in forward]
        low = lax.ppermute(
            lax.slice_in_dim(block, block.shape[dim] - width, None, axis=dim), axis, forward
        )
        high = lax.ppermute(lax.slice_in_dim(block, 0, width, axis=dim), axis, backward)
        block = jnp.concatenate([low, block, high], axis=dim)
    return block


def shifted(array, axis, by):
    devices = lax.axis_size(axis)
    pairs = [(i, i + by) for i in range(devices) if 0 <= i + by < devices]
    return lax.ppermute(array, axis, pairs)


def harmonic_table(azimuth, harmonic, count_all):
    half_count = count_all // 2
    orders = jnp.where(harmonic <= half_count, harmonic, harmonic - half_count)
    phases = azimuth[:, None] * orders[None, :] % count_all
    angles = phases.astype(jnp.float32) * (2.0 * math.pi / count_all)
    return jnp.where(harmonic[None, :] <= half_count, jnp.cos(angles), jnp.sin(angles))


def harmonic_weight(harmonic, count_all):
    half_count = count_all // 2
    edge_mode = (harmonic == 0) | (harmonic == half_count)
    return jnp.where(edge_mode, 1.0 / count_all, 2.0 / count_all).astype(jnp.float32)


def harmonic_order(harmonic, count_all):
    half_count = count_all // 2
    return jnp.where(harmonic <= half_count, harmonic, harmonic - half_count).astype(jnp.float32)


def radial_profiles(radial_count, band_start, band_width):
    cell_index = jnp.arange(radial_count, dtype=jnp.int32)
    radius = R_CORE + cell_index.astype(jnp.float32)
    inside = (cell_index >= band_start) & (cell_index < band_start + band_width)
    conduct = jnp.where(inside, KAPPA, AIR_TERM).astype(jnp.float32)
    coil_zone = (cell_index < band_start).astype(jnp.float32)
    return (radius, conduct, coil_zone)


def radial_sum(iterate):
    radial_pad = jnp.pad(iterate, ((0, 0), (0, 0), (1, 1)))
    return radial_pad[:, :, 2:] + radial_pad[:, :, :-2]


def lorentz(padded, previous, conduct, radius, band_start, band_width):
    current_field = padded[:, 1:-1]
    axial_slope = (padded[:, 2:] - padded[:, :-2]) * 0.5
    radial_pad = jnp.pad(current_field, ((0, 0), (0, 0), (1, 1)))
    radial_slope = (radial_pad[:, :, 2:] - radial_pad[:, :, :-2]) * 0.5
    b_axial = radial_slope + current_field / radius
    eddy_current = -conduct * (current_field - previous)
    force_radial = FORCE_K * eddy_current * b_axial
    force_axial = FORCE_K * eddy_current * axial_slope
    return jnp.concatenate(
        [
            force_radial[..., band_start : band_start + band_width],
            force_axial[..., band_start : band_start + band_width],
        ],
        axis=-1,
    )


def plastic_update(load, velocity, strain, plastic):
    trial_stress = E_MOD * (strain - plastic)
    excess = jnp.abs(trial_stress) - YIELD_ZERO
    increment = (
        trial_stress
        * jnp.maximum(excess, 0.0)
        / ((E_MOD + HARDEN) * jnp.maximum(jnp.abs(trial_stress), YIELD_ZERO))
    )
    plastic = plastic + increment
    stress = E_MOD * (strain - plastic)
    velocity = DAMPING * velocity + TIME_STEP * (load - STIFFNESS * stress)
    strain = strain + TIME_STEP * velocity
    return (velocity, strain, plastic)


def basis_constant(count_all):
    half_count = count_all // 2
    harmonic = np.arange(count_all)
    orders = np.where(harmonic <= half_count, harmonic, harmonic - half_count)
    phases = (harmonic[:, None] * orders[None, :]) % count_all
    angles = phases.astype(np.float64) * (2.0 * math.pi / count_all)
    table = np.where(harmonic[None, :] <= half_count, np.cos(angles), np.sin(angles))
    return table.astype(np.float32)


def transform(main, rest, basis, inverse):
    devices, rows, lanes = main.shape
    count = rest.shape[1]
    unit = devices * lanes // math.gcd(rows, lanes)
    padded = -(-count // unit) * unit
    width = padded // devices
    packed = (devices, rows * width // lanes, lanes)
    rest = jnp.pad(rest, ((0, 0), (0, padded - count)))
    rest = rest.reshape(rows, devices, width).transpose(1, 0, 2).reshape(packed)
    spread = lax.all_to_all(
        jnp.concatenate([main, rest], axis=1), "azim", 0, 0, tiled=True
    )
    contract = 1 if inverse else 0

    def mix(columns):
        return lax.dot_general(
            basis, columns, (((contract,), (0,)), ((), ())), precision=lax.Precision.HIGH,
            preferred_element_type=jnp.float32,
        )

    mixed = mix(
        jnp.concatenate(
            [
                spread[:, :rows].reshape(devices * rows, lanes),
                spread[:, rows:].reshape(devices * rows, width),
            ],
            axis=1,
        )
    )
    mixed_main = mixed[:, :lanes].reshape(main.shape)
    mixed_rest = mixed[:, lanes:].reshape(packed)
    joined = lax.all_to_all(
        jnp.concatenate([mixed_main, mixed_rest], axis=1), "azim", 0, 0, tiled=True
    )
    rest = joined[:, rows:].reshape(devices, rows, width).transpose(1, 0, 2)
    return joined[:, :rows], rest.reshape(rows, padded)[:, :count]


def lorentz_window(padded, previous, conduct, radius):
    current_field = padded[:, 1:-1]
    axial_slope = (padded[:, 2:] - padded[:, :-2]) * 0.5
    radial_pad = jnp.pad(current_field, ((0, 0), (0, 0), (1, 1)))
    radial_slope = (radial_pad[:, :, 2:] - radial_pad[:, :, :-2]) * 0.5
    b_axial = radial_slope + current_field / radius
    eddy_current = -conduct * (current_field - previous)
    force_radial = FORCE_K * eddy_current * b_axial
    force_axial = FORCE_K * eddy_current * axial_slope
    return jnp.concatenate([force_radial[..., 1:-1], force_axial[..., 1:-1]], axis=-1)


def shards(
    coil_density,
    coil_mask,
    drive,
    potential,
    tile_weight,
    relay_owner,
    relay_slot,
    velocity,
    strain,
    plastic,
):
    local_count, axial_cells, radial_cells = potential.shape
    band_width = tile_weight.shape[1]
    azim_total = local_count * lax.axis_size("azim")
    own_index = lax.axis_index("azim") * local_count + jnp.arange(local_count, dtype=jnp.int32)
    band_start = radial_cells // 4
    radius, conduct, coil_zone = radial_profiles(radial_cells, band_start, band_width)
    orders = harmonic_order(own_index, azim_total)
    diagonal_term = (
        4.0 + conduct[None, None, :] + (orders[:, None, None] / radius[None, None, :]) ** 2
    )
    basis = jnp.asarray(basis_constant(azim_total))

    coil = coil_density[..., :band_start] * coil_mask[..., :band_start].astype(jnp.float32)
    field_modes, coil_modes = transform(
        potential.transpose(1, 0, 2), coil.reshape(local_count, -1), basis, inverse=False
    )
    modes = jnp.concatenate(
        [
            field_modes.transpose(1, 0, 2),
            coil_modes.reshape(local_count, axial_cells, band_start),
        ],
        axis=-1,
    )

    reach = STEPS * SWEEPS + 1
    modes = with_halo(modes, (("axial", 1),), reach)
    field_modes = modes[..., :radial_cells]
    coil_modes = jnp.pad(modes[..., radial_cells:], ((0, 0), (0, 0), (0, radial_cells - band_start)))
    span = axial_cells + 2 * reach
    global_z = lax.axis_index("axial") * axial_cells - reach + jnp.arange(span, dtype=jnp.int32)
    inside = ((global_z >= 0) & (global_z < axial_cells * lax.axis_size("axial")))[None, :, None]
    divisor = jnp.where(inside, diagonal_term, jnp.inf)

    weight = harmonic_weight(own_index, azim_total)[:, None, None]
    window = slice(band_start - 1, band_start + band_width + 1)
    iterate = field_modes
    kept = []
    trim = 0
    for step_index in range(STEPS):
        right_side = MU_COIL * (drive[step_index] * coil_modes[:, trim : span - trim]) + (
            conduct * iterate
        )
        for sweep_index in range(SWEEPS):
            trim += 1
            nearby = iterate[:, 2:] + iterate[:, :-2] + radial_sum(iterate[:, 1:-1])
            right_side = right_side[:, 1:-1]
            iterate = (right_side + nearby) / divisor[:, trim : span - trim]
        kept.append(iterate[:, reach - 1 - trim : reach - trim + axial_cells + 1] * weight)
    last = kept[-1]
    edges = jnp.concatenate([last[:, :1], last[:, -1:]], axis=1)[..., window]
    pieces = [edges.shape] + [piece[..., window].shape for piece in kept[:-1]]
    extra = jnp.concatenate(
        [edges.reshape(local_count, -1)]
        + [piece[..., window].reshape(local_count, -1) for piece in kept[:-1]],
        axis=1,
    )
    planes, extra = transform(last[:, 1:-1].transpose(1, 0, 2), extra, basis, inverse=True)
    field_out = planes.transpose(1, 0, 2)
    unpacked, offset = [], 0
    for shape in pieces:
        size = math.prod(shape[1:])
        unpacked.append(extra[:, offset : offset + size].reshape(shape))
        offset += size
    edges = unpacked[0]
    fields = unpacked[1:] + [
        jnp.concatenate([edges[:, :1], field_out[..., window], edges[:, 1:]], axis=1)
    ]

    previous = potential[..., window]
    tiles = []
    for step_index in range(STEPS):
        padded = fields[step_index]
        tiles.append(lorentz_window(padded, previous, conduct[window], radius[window]))
        previous = padded[:, 1:-1]
    tiles = jnp.stack(tiles)

    slot_range = jnp.arange(local_count, dtype=jnp.int32)
    slot_table = relay_slot[:, :, 0][:, :, None] == slot_range[None, None, :]
    owner_at = jnp.sum(jnp.where(slot_table, relay_owner[:, :, 0][:, :, None], 0), axis=1)
    moved = jnp.einsum(
        "sjcw,sjp->spcw", tiles, slot_table.astype(jnp.float32), precision=HIGH
    )

    blank = jnp.zeros_like(tile_weight)
    paired = jnp.concatenate(
        [
            jnp.concatenate([tile_weight, blank], axis=2),
            jnp.concatenate([blank, tile_weight], axis=2),
        ],
        axis=1,
    )
    mapped = jnp.einsum("apr,sazr->sazp", paired, moved, precision=lax.Precision.HIGH)

    def place(target):
        return jnp.where((owner_at == target)[:, :, None, None], mapped, 0.0)

    from_below = shifted(place(2), "axial", 1)
    from_above = shifted(place(0), "axial", -1)
    loads = place(1) + from_below + from_above
    for step_index in range(STEPS):
        velocity, strain, plastic = plastic_update(loads[step_index], velocity, strain, plastic)
    return (field_out, velocity, strain, plastic)


def solution(mesh):
    placed = (
        P("azim", "axial", None),
        P("azim", "axial", None),
        P(),
        P("azim", "axial", None),
        P("azim", None, None),
        P(None, "azim", "axial"),
        P(None, "azim", "axial"),
        P("azim", "axial", None),
        P("azim", "axial", None),
        P("azim", "axial", None),
    )
    return jax.shard_map(
        shards,
        mesh=mesh,
        in_specs=placed,
        out_specs=(
            P("azim", "axial", None),
            P("azim", "axial", None),
            P("azim", "axial", None),
            P("azim", "axial", None),
        ),
        check_vma=False,
    )
```

```python
import math

import jax
import numpy as np
import jax.numpy as jnp
from jax import lax
from jax.sharding import PartitionSpec as P

STEPS = 2
SWEEPS = 3


HIGH = lax.Precision.HIGHEST
KAPPA = 2.0
AIR_TERM = 0.05
R_CORE = 16.0
MU_COIL = 1.0
FORCE_K = 1.0
E_MOD = 1.0
YIELD_ZERO = 0.5
HARDEN = 0.3
TIME_STEP = 0.5
STIFFNESS = 0.5
DAMPING = 0.9


def with_halo(block, sides, width):
    for axis, dim in sides:
        count = lax.axis_size(axis)
        forward = [(i, i + 1) for i in range(count - 1)]
        backward = [(target, source) for source, target in forward]
        low = lax.ppermute(
            lax.slice_in_dim(block, block.shape[dim] - width, None, axis=dim), axis, forward
        )
        high = lax.ppermute(lax.slice_in_dim(block, 0, width, axis=dim), axis, backward)
        block = jnp.concatenate([low, block, high], axis=dim)
    return block


def shifted(array, axis, by):
    devices = lax.axis_size(axis)
    pairs = [(i, i + by) for i in range(devices) if 0 <= i + by < devices]
    return lax.ppermute(array, axis, pairs)


def harmonic_table(azimuth, harmonic, count_all):
    half_count = count_all // 2
    orders = jnp.where(harmonic <= half_count, harmonic, harmonic - half_count)
    phases = azimuth[:, None] * orders[None, :] % count_all
    angles = phases.astype(jnp.float32) * (2.0 * math.pi / count_all)
    return jnp.where(harmonic[None, :] <= half_count, jnp.cos(angles), jnp.sin(angles))


def harmonic_weight(harmonic, count_all):
    half_count = count_all // 2
    edge_mode = (harmonic == 0) | (harmonic == half_count)
    return jnp.where(edge_mode, 1.0 / count_all, 2.0 / count_all).astype(jnp.float32)


def harmonic_order(harmonic, count_all):
    half_count = count_all // 2
    return jnp.where(harmonic <= half_count, harmonic, harmonic - half_count).astype(jnp.float32)


def radial_profiles(radial_count, band_start, band_width):
    cell_index = jnp.arange(radial_count, dtype=jnp.int32)
    radius = R_CORE + cell_index.astype(jnp.float32)
    inside = (cell_index >= band_start) & (cell_index < band_start + band_width)
    conduct = jnp.where(inside, KAPPA, AIR_TERM).astype(jnp.float32)
    coil_zone = (cell_index < band_start).astype(jnp.float32)
    return (radius, conduct, coil_zone)


def radial_sum(iterate):
    radial_pad = jnp.pad(iterate, ((0, 0), (0, 0), (1, 1)))
    return radial_pad[:, :, 2:] + radial_pad[:, :, :-2]


def lorentz(padded, previous, conduct, radius, band_start, band_width):
    current_field = padded[:, 1:-1]
    axial_slope = (padded[:, 2:] - padded[:, :-2]) * 0.5
    radial_pad = jnp.pad(current_field, ((0, 0), (0, 0), (1, 1)))
    radial_slope = (radial_pad[:, :, 2:] - radial_pad[:, :, :-2]) * 0.5
    b_axial = radial_slope + current_field / radius
    eddy_current = -conduct * (current_field - previous)
    force_radial = FORCE_K * eddy_current * b_axial
    force_axial = FORCE_K * eddy_current * axial_slope
    return jnp.concatenate(
        [
            force_radial[..., band_start : band_start + band_width],
            force_axial[..., band_start : band_start + band_width],
        ],
        axis=-1,
    )


def plastic_update(load, velocity, strain, plastic):
    trial_stress = E_MOD * (strain - plastic)
    excess = jnp.abs(trial_stress) - YIELD_ZERO
    increment = (
        trial_stress
        * jnp.maximum(excess, 0.0)
        / ((E_MOD + HARDEN) * jnp.maximum(jnp.abs(trial_stress), YIELD_ZERO))
    )
    plastic = plastic + increment
    stress = E_MOD * (strain - plastic)
    velocity = DAMPING * velocity + TIME_STEP * (load - STIFFNESS * stress)
    strain = strain + TIME_STEP * velocity
    return (velocity, strain, plastic)


def basis_constant(count_all):
    half_count = count_all // 2
    harmonic = np.arange(count_all)
    orders = np.where(harmonic <= half_count, harmonic, harmonic - half_count)
    phases = (harmonic[:, None] * orders[None, :]) % count_all
    angles = phases.astype(np.float64) * (2.0 * math.pi / count_all)
    table = np.where(harmonic[None, :] <= half_count, np.cos(angles), np.sin(angles))
    return table.astype(np.float32)


def transform(main, rest, basis, inverse):
    devices, rows, lanes = main.shape
    count = rest.shape[1]
    unit = devices * lanes // math.gcd(rows, lanes)
    padded = -(-count // unit) * unit
    width = padded // devices
    packed = (devices, rows * width // lanes, lanes)
    rest = jnp.pad(rest, ((0, 0), (0, padded - count)))
    rest = rest.reshape(rows, devices, width).transpose(1, 0, 2).reshape(packed)
    spread = lax.all_to_all(
        jnp.concatenate([main, rest], axis=1), "azim", 0, 0, tiled=True
    )
    contract = 1 if inverse else 0

    def mix(columns):
        return lax.dot_general(
            basis, columns, (((contract,), (0,)), ((), ())), precision=lax.Precision.HIGH,
            preferred_element_type=jnp.float32,
        )

    mixed = mix(
        jnp.concatenate(
            [
                spread[:, :rows].reshape(devices * rows, lanes),
                spread[:, rows:].reshape(devices * rows, width),
            ],
            axis=1,
        )
    )
    mixed_main = mixed[:, :lanes].reshape(main.shape)
    mixed_rest = mixed[:, lanes:].reshape(packed)
    joined = lax.all_to_all(
        jnp.concatenate([mixed_main, mixed_rest], axis=1), "azim", 0, 0, tiled=True
    )
    rest = joined[:, rows:].reshape(devices, rows, width).transpose(1, 0, 2)
    return joined[:, :rows], rest.reshape(rows, padded)[:, :count]


def lorentz_window(padded, previous, conduct, radius):
    current_field = padded[:, 1:-1]
    axial_slope = (padded[:, 2:] - padded[:, :-2]) * 0.5
    radial_pad = jnp.pad(current_field, ((0, 0), (0, 0), (1, 1)))
    radial_slope = (radial_pad[:, :, 2:] - radial_pad[:, :, :-2]) * 0.5
    b_axial = radial_slope + current_field / radius
    eddy_current = -conduct * (current_field - previous)
    force_radial = FORCE_K * eddy_current * b_axial
    force_axial = FORCE_K * eddy_current * axial_slope
    return jnp.concatenate([force_radial[..., 1:-1], force_axial[..., 1:-1]], axis=-1)


def shards(
    coil_density,
    coil_mask,
    drive,
    potential,
    tile_weight,
    relay_owner,
    relay_slot,
    velocity,
    strain,
    plastic,
):
    local_count, axial_cells, radial_cells = potential.shape
    band_width = tile_weight.shape[1]
    azim_total = local_count * lax.axis_size("azim")
    own_index = lax.axis_index("azim") * local_count + jnp.arange(local_count, dtype=jnp.int32)
    band_start = radial_cells // 4
    radius, conduct, coil_zone = radial_profiles(radial_cells, band_start, band_width)
    orders = harmonic_order(own_index, azim_total)
    diagonal_term = (
        4.0 + conduct[None, None, :] + (orders[:, None, None] / radius[None, None, :]) ** 2
    )
    basis = jnp.asarray(basis_constant(azim_total))

    coil = coil_density[..., :band_start] * coil_mask[..., :band_start].astype(jnp.float32)
    field_modes, coil_modes = transform(
        potential.transpose(1, 0, 2), coil.reshape(local_count, -1), basis, inverse=False
    )
    modes = jnp.concatenate(
        [
            field_modes.transpose(1, 0, 2),
            coil_modes.reshape(local_count, axial_cells, band_start),
        ],
        axis=-1,
    )

    reach = STEPS * SWEEPS + 1
    modes = with_halo(modes, (("axial", 1),), reach)
    field_modes = modes[..., :radial_cells]
    coil_modes = jnp.pad(modes[..., radial_cells:], ((0, 0), (0, 0), (0, radial_cells - band_start)))
    span = axial_cells + 2 * reach
    global_z = lax.axis_index("axial") * axial_cells - reach + jnp.arange(span, dtype=jnp.int32)
    inside = ((global_z >= 0) & (global_z < axial_cells * lax.axis_size("axial")))[None, :, None]
    divisor = jnp.where(inside, diagonal_term, jnp.inf)

    weight = harmonic_weight(own_index, azim_total)[:, None, None]
    window = slice(band_start - 1, band_start + band_width + 1)
    iterate = field_modes
    kept = []
    for step_index in range(STEPS):
        right_side = MU_COIL * (drive[step_index] * coil_modes) + conduct * iterate
        for sweep_index in range(SWEEPS):
            axial_pad = jnp.pad(iterate, ((0, 0), (1, 1), (0, 0)))
            nearby = axial_pad[:, 2:] + axial_pad[:, :-2] + radial_sum(iterate)
            iterate = (right_side + nearby) / divisor
        kept.append(iterate[:, reach - 1 : reach + axial_cells + 1] * weight)
    last = kept[-1]
    edges = jnp.concatenate([last[:, :1], last[:, -1:]], axis=1)[..., window]
    pieces = [edges.shape] + [piece[..., window].shape for piece in kept[:-1]]
    extra = jnp.concatenate(
        [edges.reshape(local_count, -1)]
        + [piece[..., window].reshape(local_count, -1) for piece in kept[:-1]],
        axis=1,
    )
    planes, extra = transform(last[:, 1:-1].transpose(1, 0, 2), extra, basis, inverse=True)
    field_out = planes.transpose(1, 0, 2)
    unpacked, offset = [], 0
    for shape in pieces:
        size = math.prod(shape[1:])
        unpacked.append(extra[:, offset : offset + size].reshape(shape))
        offset += size
    edges = unpacked[0]
    fields = unpacked[1:] + [
        jnp.concatenate([edges[:, :1], field_out[..., window], edges[:, 1:]], axis=1)
    ]

    previous = potential[..., window]
    tiles = []
    for step_index in range(STEPS):
        padded = fields[step_index]
        tiles.append(lorentz_window(padded, previous, conduct[window], radius[window]))
        previous = padded[:, 1:-1]
    tiles = jnp.stack(tiles)

    slot_range = jnp.arange(local_count, dtype=jnp.int32)
    slot_table = relay_slot[:, :, 0][:, :, None] == slot_range[None, None, :]
    owner_at = jnp.sum(jnp.where(slot_table, relay_owner[:, :, 0][:, :, None], 0), axis=1)
    moved = jnp.einsum(
        "sjcw,sjp->spcw", tiles, slot_table.astype(jnp.float32), precision=HIGH
    )

    blank = jnp.zeros_like(tile_weight)
    paired = jnp.concatenate(
        [
            jnp.concatenate([tile_weight, blank], axis=2),
            jnp.concatenate([blank, tile_weight], axis=2),
        ],
        axis=1,
    )
    mapped = jnp.einsum("apr,sazr->sazp", paired, moved, precision=lax.Precision.HIGH)

    def place(target):
        return jnp.where((owner_at == target)[:, :, None, None], mapped, 0.0)

    from_below = shifted(place(2), "axial", 1)
    from_above = shifted(place(0), "axial", -1)
    loads = place(1) + from_below + from_above
    trial_stress = E_MOD * (strain - plastic)
    excess = jnp.abs(trial_stress) - YIELD_ZERO
    increment = (
        trial_stress
        * jnp.maximum(excess, 0.0)
        / ((E_MOD + HARDEN) * jnp.maximum(jnp.abs(trial_stress), YIELD_ZERO))
    )
    plastic = plastic + increment
    stress = E_MOD * (strain - plastic)
    damped, stress = lax.optimization_barrier((DAMPING * velocity, STIFFNESS * stress))
    velocity = damped + TIME_STEP * (loads[0] - stress)
    strain = strain + TIME_STEP * velocity
    for step_index in range(1, STEPS):
        velocity, strain, plastic = plastic_update(loads[step_index], velocity, strain, plastic)
    return (field_out, velocity, strain, plastic)


def solution(mesh):
    placed = (
        P("azim", "axial", None),
        P("azim", "axial", None),
        P(),
        P("azim", "axial", None),
        P("azim", None, None),
        P(None, "azim", "axial"),
        P(None, "azim", "axial"),
        P("azim", "axial", None),
        P("azim", "axial", None),
        P("azim", "axial", None),
    )
    return jax.shard_map(
        shards,
        mesh=mesh,
        in_specs=placed,
        out_specs=(
            P("azim", "axial", None),
            P("azim", "axial", None),
            P("azim", "axial", None),
            P("azim", "axial", None),
        ),
        check_vma=False,
    )
```

```python
import math

import jax
import numpy as np
import jax.numpy as jnp
from jax import lax
from jax.sharding import PartitionSpec as P

STEPS = 2
SWEEPS = 3


HIGH = lax.Precision.HIGHEST
KAPPA = 2.0
AIR_TERM = 0.05
R_CORE = 16.0
MU_COIL = 1.0
FORCE_K = 1.0
E_MOD = 1.0
YIELD_ZERO = 0.5
HARDEN = 0.3
TIME_STEP = 0.5
STIFFNESS = 0.5
DAMPING = 0.9


def with_halo(block, sides, width):
    for axis, dim in sides:
        count = lax.axis_size(axis)
        forward = [(i, i + 1) for i in range(count - 1)]
        backward = [(target, source) for source, target in forward]
        low = lax.ppermute(
            lax.slice_in_dim(block, block.shape[dim] - width, None, axis=dim), axis, forward
        )
        high = lax.ppermute(lax.slice_in_dim(block, 0, width, axis=dim), axis, backward)
        block = jnp.concatenate([low, block, high], axis=dim)
    return block


def shifted(array, axis, by):
    devices = lax.axis_size(axis)
    pairs = [(i, i + by) for i in range(devices) if 0 <= i + by < devices]
    return lax.ppermute(array, axis, pairs)


def harmonic_table(azimuth, harmonic, count_all):
    half_count = count_all // 2
    orders = jnp.where(harmonic <= half_count, harmonic, harmonic - half_count)
    phases = azimuth[:, None] * orders[None, :] % count_all
    angles = phases.astype(jnp.float32) * (2.0 * math.pi / count_all)
    return jnp.where(harmonic[None, :] <= half_count, jnp.cos(angles), jnp.sin(angles))


def harmonic_weight(harmonic, count_all):
    half_count = count_all // 2
    edge_mode = (harmonic == 0) | (harmonic == half_count)
    return jnp.where(edge_mode, 1.0 / count_all, 2.0 / count_all).astype(jnp.float32)


def harmonic_order(harmonic, count_all):
    half_count = count_all // 2
    return jnp.where(harmonic <= half_count, harmonic, harmonic - half_count).astype(jnp.float32)


def radial_profiles(radial_count, band_start, band_width):
    cell_index = jnp.arange(radial_count, dtype=jnp.int32)
    radius = R_CORE + cell_index.astype(jnp.float32)
    inside = (cell_index >= band_start) & (cell_index < band_start + band_width)
    conduct = jnp.where(inside, KAPPA, AIR_TERM).astype(jnp.float32)
    coil_zone = (cell_index < band_start).astype(jnp.float32)
    return (radius, conduct, coil_zone)


def radial_sum(iterate):
    radial_pad = jnp.pad(iterate, ((0, 0), (0, 0), (1, 1)))
    return radial_pad[:, :, 2:] + radial_pad[:, :, :-2]


def lorentz(padded, previous, conduct, radius, band_start, band_width):
    current_field = padded[:, 1:-1]
    axial_slope = (padded[:, 2:] - padded[:, :-2]) * 0.5
    radial_pad = jnp.pad(current_field, ((0, 0), (0, 0), (1, 1)))
    radial_slope = (radial_pad[:, :, 2:] - radial_pad[:, :, :-2]) * 0.5
    b_axial = radial_slope + current_field / radius
    eddy_current = -conduct * (current_field - previous)
    force_radial = FORCE_K * eddy_current * b_axial
    force_axial = FORCE_K * eddy_current * axial_slope
    return jnp.concatenate(
        [
            force_radial[..., band_start : band_start + band_width],
            force_axial[..., band_start : band_start + band_width],
        ],
        axis=-1,
    )


def plastic_update(load, velocity, strain, plastic):
    trial_stress = E_MOD * (strain - plastic)
    excess = jnp.abs(trial_stress) - YIELD_ZERO
    increment = (
        trial_stress
        * jnp.maximum(excess, 0.0)
        / ((E_MOD + HARDEN) * jnp.maximum(jnp.abs(trial_stress), YIELD_ZERO))
    )
    plastic = plastic + increment
    stress = E_MOD * (strain - plastic)
    velocity = DAMPING * velocity + TIME_STEP * (load - STIFFNESS * stress)
    strain = strain + TIME_STEP * velocity
    return (velocity, strain, plastic)


def basis_constant(count_all):
    half_count = count_all // 2
    harmonic = np.arange(count_all)
    orders = np.where(harmonic <= half_count, harmonic, harmonic - half_count)
    phases = (harmonic[:, None] * orders[None, :]) % count_all
    angles = phases.astype(np.float64) * (2.0 * math.pi / count_all)
    table = np.where(harmonic[None, :] <= half_count, np.cos(angles), np.sin(angles))
    return table.astype(np.float32)


def transform(main, rest, basis, inverse):
    devices, rows, lanes = main.shape
    count = rest.shape[1]
    unit = devices * lanes // math.gcd(rows, lanes)
    padded = -(-count // unit) * unit
    width = padded // devices
    packed = (devices, rows * width // lanes, lanes)
    rest = jnp.pad(rest, ((0, 0), (0, padded - count)))
    rest = rest.reshape(rows, devices, width).transpose(1, 0, 2).reshape(packed)
    spread = lax.all_to_all(
        jnp.concatenate([main, rest], axis=1), "azim", 0, 0, tiled=True
    )
    contract = 1 if inverse else 0

    def mix(columns):
        return lax.dot_general(
            basis, columns, (((contract,), (0,)), ((), ())), precision=lax.Precision.HIGH,
            preferred_element_type=jnp.float32,
        )

    mixed = mix(
        jnp.concatenate(
            [
                spread[:, :rows].reshape(devices * rows, lanes),
                spread[:, rows:].reshape(devices * rows, width),
            ],
            axis=1,
        )
    )
    mixed_main = mixed[:, :lanes].reshape(main.shape)
    mixed_rest = mixed[:, lanes:].reshape(packed)
    joined = lax.all_to_all(
        jnp.concatenate([mixed_main, mixed_rest], axis=1), "azim", 0, 0, tiled=True
    )
    rest = joined[:, rows:].reshape(devices, rows, width).transpose(1, 0, 2)
    return joined[:, :rows], rest.reshape(rows, padded)[:, :count]


def lorentz_window(padded, previous, conduct, radius):
    current_field = padded[:, 1:-1]
    axial_slope = (padded[:, 2:] - padded[:, :-2]) * 0.5
    radial_pad = jnp.pad(current_field, ((0, 0), (0, 0), (1, 1)))
    radial_slope = (radial_pad[:, :, 2:] - radial_pad[:, :, :-2]) * 0.5
    b_axial = radial_slope + current_field / radius
    eddy_current = -conduct * (current_field - previous)
    force_radial = FORCE_K * eddy_current * b_axial
    force_axial = FORCE_K * eddy_current * axial_slope
    return jnp.concatenate([force_radial[..., 1:-1], force_axial[..., 1:-1]], axis=-1)


def shards(
    coil_density,
    coil_mask,
    drive,
    potential,
    tile_weight,
    relay_owner,
    relay_slot,
    velocity,
    strain,
    plastic,
):
    local_count, axial_cells, radial_cells = potential.shape
    band_width = tile_weight.shape[1]
    azim_total = local_count * lax.axis_size("azim")
    own_index = lax.axis_index("azim") * local_count + jnp.arange(local_count, dtype=jnp.int32)
    band_start = radial_cells // 4
    radius, conduct, coil_zone = radial_profiles(radial_cells, band_start, band_width)
    orders = harmonic_order(own_index, azim_total)
    diagonal_term = (
        4.0 + conduct[None, None, :] + (orders[:, None, None] / radius[None, None, :]) ** 2
    )
    basis = jnp.asarray(basis_constant(azim_total))

    coil = coil_density[..., :band_start] * coil_mask[..., :band_start].astype(jnp.float32)
    field_modes, coil_modes = transform(
        potential.transpose(1, 0, 2), coil.reshape(local_count, -1), basis, inverse=False
    )
    modes = jnp.concatenate(
        [
            field_modes.transpose(1, 0, 2),
            coil_modes.reshape(local_count, axial_cells, band_start),
        ],
        axis=-1,
    )

    reach = STEPS * SWEEPS + 1
    modes = with_halo(modes, (("axial", 1),), reach)
    field_modes = modes[..., :radial_cells]
    coil_modes = jnp.pad(modes[..., radial_cells:], ((0, 0), (0, 0), (0, radial_cells - band_start)))
    span = axial_cells + 2 * reach
    global_z = lax.axis_index("axial") * axial_cells - reach + jnp.arange(span, dtype=jnp.int32)
    inside = ((global_z >= 0) & (global_z < axial_cells * lax.axis_size("axial")))[None, :, None]
    divisor = jnp.where(inside, diagonal_term, jnp.inf)

    weight = harmonic_weight(own_index, azim_total)[:, None, None]
    window = slice(band_start - 1, band_start + band_width + 1)
    iterate = field_modes
    kept = []
    for step_index in range(STEPS):
        right_side = MU_COIL * (drive[step_index] * coil_modes) + conduct * iterate
        for sweep_index in range(SWEEPS):
            axial_pad = jnp.pad(iterate, ((0, 0), (1, 1), (0, 0)))
            nearby = axial_pad[:, 2:] + axial_pad[:, :-2] + radial_sum(iterate)
            iterate = (right_side + nearby) / divisor
        kept.append(iterate[:, reach - 1 : reach + axial_cells + 1] * weight)
    last = kept[-1]
    edges = jnp.concatenate([last[:, :1], last[:, -1:]], axis=1)[..., window]
    pieces = [edges.shape] + [piece[..., window].shape for piece in kept[:-1]]
    extra = jnp.concatenate(
        [edges.reshape(local_count, -1)]
        + [piece[..., window].reshape(local_count, -1) for piece in kept[:-1]],
        axis=1,
    )
    planes, extra = transform(last[:, 1:-1].transpose(1, 0, 2), extra, basis, inverse=True)
    field_out = planes.transpose(1, 0, 2)
    unpacked, offset = [], 0
    for shape in pieces:
        size = math.prod(shape[1:])
        unpacked.append(extra[:, offset : offset + size].reshape(shape))
        offset += size
    edges = unpacked[0]
    fields = unpacked[1:] + [
        jnp.concatenate([edges[:, :1], field_out[..., window], edges[:, 1:]], axis=1)
    ]

    previous = potential[..., window]
    tiles = []
    for step_index in range(STEPS):
        padded = fields[step_index]
        tiles.append(lorentz_window(padded, previous, conduct[window], radius[window]))
        previous = padded[:, 1:-1]
    tiles = jnp.stack(tiles)

    slot_range = jnp.arange(local_count, dtype=jnp.int32)
    slot_table = relay_slot[:, :, 0][:, :, None] == slot_range[None, None, :]
    owner_at = jnp.sum(jnp.where(slot_table, relay_owner[:, :, 0][:, :, None], 0), axis=1)
    moved = jnp.einsum(
        "sjcw,sjp->spcw", tiles, slot_table.astype(jnp.float32), precision=lax.Precision.HIGH
    )

    blank = jnp.zeros_like(tile_weight)
    paired = jnp.concatenate(
        [
            jnp.concatenate([tile_weight, blank], axis=2),
            jnp.concatenate([blank, tile_weight], axis=2),
        ],
        axis=1,
    )
    mapped = jnp.einsum("apr,sazr->sazp", paired, moved, precision=lax.Precision.HIGH)

    def place(target):
        return jnp.where((owner_at == target)[:, :, None, None], mapped, 0.0)

    from_below = shifted(place(2), "axial", 1)
    from_above = shifted(place(0), "axial", -1)
    loads = place(1) + from_below + from_above
    trial_stress = E_MOD * (strain - plastic)
    excess = jnp.abs(trial_stress) - YIELD_ZERO
    increment = (
        trial_stress
        * jnp.maximum(excess, 0.0)
        / ((E_MOD + HARDEN) * jnp.maximum(jnp.abs(trial_stress), YIELD_ZERO))
    )
    plastic = plastic + increment
    stress = E_MOD * (strain - plastic)
    damped, stress = lax.optimization_barrier((DAMPING * velocity, STIFFNESS * stress))
    velocity = damped + TIME_STEP * (loads[0] - stress)
    strain = strain + TIME_STEP * velocity
    for step_index in range(1, STEPS):
        velocity, strain, plastic = plastic_update(loads[step_index], velocity, strain, plastic)
    return (field_out, velocity, strain, plastic)


def solution(mesh):
    placed = (
        P("azim", "axial", None),
        P("azim", "axial", None),
        P(),
        P("azim", "axial", None),
        P("azim", None, None),
        P(None, "azim", "axial"),
        P(None, "azim", "axial"),
        P("azim", "axial", None),
        P("azim", "axial", None),
        P("azim", "axial", None),
    )
    return jax.shard_map(
        shards,
        mesh=mesh,
        in_specs=placed,
        out_specs=(
            P("azim", "axial", None),
            P("azim", "axial", None),
            P("azim", "axial", None),
            P("azim", "axial", None),
        ),
        check_vma=False,
    )
```

```python
import math

import jax
import numpy as np
import jax.numpy as jnp
from jax import lax
from jax.sharding import PartitionSpec as P

STEPS = 2
SWEEPS = 3


HIGH = lax.Precision.HIGHEST
KAPPA = 2.0
AIR_TERM = 0.05
R_CORE = 16.0
MU_COIL = 1.0
FORCE_K = 1.0
E_MOD = 1.0
YIELD_ZERO = 0.5
HARDEN = 0.3
TIME_STEP = 0.5
STIFFNESS = 0.5
DAMPING = 0.9


def with_halo(block, sides, width):
    for axis, dim in sides:
        count = lax.axis_size(axis)
        forward = [(i, i + 1) for i in range(count - 1)]
        backward = [(target, source) for source, target in forward]
        low = lax.ppermute(
            lax.slice_in_dim(block, block.shape[dim] - width, None, axis=dim), axis, forward
        )
        high = lax.ppermute(lax.slice_in_dim(block, 0, width, axis=dim), axis, backward)
        block = jnp.concatenate([low, block, high], axis=dim)
    return block


def shifted(array, axis, by):
    devices = lax.axis_size(axis)
    pairs = [(i, i + by) for i in range(devices) if 0 <= i + by < devices]
    return lax.ppermute(array, axis, pairs)


def harmonic_table(azimuth, harmonic, count_all):
    half_count = count_all // 2
    orders = jnp.where(harmonic <= half_count, harmonic, harmonic - half_count)
    phases = azimuth[:, None] * orders[None, :] % count_all
    angles = phases.astype(jnp.float32) * (2.0 * math.pi / count_all)
    return jnp.where(harmonic[None, :] <= half_count, jnp.cos(angles), jnp.sin(angles))


def harmonic_weight(harmonic, count_all):
    half_count = count_all // 2
    edge_mode = (harmonic == 0) | (harmonic == half_count)
    return jnp.where(edge_mode, 1.0 / count_all, 2.0 / count_all).astype(jnp.float32)


def harmonic_order(harmonic, count_all):
    half_count = count_all // 2
    return jnp.where(harmonic <= half_count, harmonic, harmonic - half_count).astype(jnp.float32)


def radial_profiles(radial_count, band_start, band_width):
    cell_index = jnp.arange(radial_count, dtype=jnp.int32)
    radius = R_CORE + cell_index.astype(jnp.float32)
    inside = (cell_index >= band_start) & (cell_index < band_start + band_width)
    conduct = jnp.where(inside, KAPPA, AIR_TERM).astype(jnp.float32)
    coil_zone = (cell_index < band_start).astype(jnp.float32)
    return (radius, conduct, coil_zone)


def radial_sum(iterate):
    radial_pad = jnp.pad(iterate, ((0, 0), (0, 0), (1, 1)))
    return radial_pad[:, :, 2:] + radial_pad[:, :, :-2]


def lorentz(padded, previous, conduct, radius, band_start, band_width):
    current_field = padded[:, 1:-1]
    axial_slope = (padded[:, 2:] - padded[:, :-2]) * 0.5
    radial_pad = jnp.pad(current_field, ((0, 0), (0, 0), (1, 1)))
    radial_slope = (radial_pad[:, :, 2:] - radial_pad[:, :, :-2]) * 0.5
    b_axial = radial_slope + current_field / radius
    eddy_current = -conduct * (current_field - previous)
    force_radial = FORCE_K * eddy_current * b_axial
    force_axial = FORCE_K * eddy_current * axial_slope
    return jnp.concatenate(
        [
            force_radial[..., band_start : band_start + band_width],
            force_axial[..., band_start : band_start + band_width],
        ],
        axis=-1,
    )


def plastic_update(load, velocity, strain, plastic):
    trial_stress = E_MOD * (strain - plastic)
    excess = jnp.abs(trial_stress) - YIELD_ZERO
    increment = (
        trial_stress
        * jnp.maximum(excess, 0.0)
        / ((E_MOD + HARDEN) * jnp.maximum(jnp.abs(trial_stress), YIELD_ZERO))
    )
    plastic = plastic + increment
    stress = E_MOD * (strain - plastic)
    velocity = DAMPING * velocity + TIME_STEP * (load - STIFFNESS * stress)
    strain = strain + TIME_STEP * velocity
    return (velocity, strain, plastic)


def basis_constant(count_all):
    half_count = count_all // 2
    harmonic = np.arange(count_all)
    orders = np.where(harmonic <= half_count, harmonic, harmonic - half_count)
    phases = (harmonic[:, None] * orders[None, :]) % count_all
    angles = phases.astype(np.float64) * (2.0 * math.pi / count_all)
    table = np.where(harmonic[None, :] <= half_count, np.cos(angles), np.sin(angles))
    return table.astype(np.float32)


def transform(main, rest, basis, inverse):
    devices, rows, lanes = main.shape
    count = rest.shape[1]
    unit = devices * lanes // math.gcd(rows, lanes)
    padded = -(-count // unit) * unit
    width = padded // devices
    packed = (devices, rows * width // lanes, lanes)
    rest = jnp.pad(rest, ((0, 0), (0, padded - count)))
    rest = rest.reshape(rows, devices, width).transpose(1, 0, 2).reshape(packed)
    spread = lax.all_to_all(
        jnp.concatenate([main, rest], axis=1), "azim", 0, 0, tiled=True
    )
    contract = 1 if inverse else 0

    def mix(columns):
        return lax.dot_general(
            basis, columns, (((contract,), (0,)), ((), ())), precision=lax.Precision.HIGH,
            preferred_element_type=jnp.float32,
        )

    mixed = mix(
        jnp.concatenate(
            [
                spread[:, :rows].reshape(devices * rows, lanes),
                spread[:, rows:].reshape(devices * rows, width),
            ],
            axis=1,
        )
    )
    mixed_main = mixed[:, :lanes].reshape(main.shape)
    mixed_rest = mixed[:, lanes:].reshape(packed)
    joined = lax.all_to_all(
        jnp.concatenate([mixed_main, mixed_rest], axis=1), "azim", 0, 0, tiled=True
    )
    rest = joined[:, rows:].reshape(devices, rows, width).transpose(1, 0, 2)
    return joined[:, :rows], rest.reshape(rows, padded)[:, :count]


def lorentz_window(padded, previous, conduct, radius):
    current_field = padded[:, 1:-1]
    axial_slope = (padded[:, 2:] - padded[:, :-2]) * 0.5
    radial_pad = jnp.pad(current_field, ((0, 0), (0, 0), (1, 1)))
    radial_slope = (radial_pad[:, :, 2:] - radial_pad[:, :, :-2]) * 0.5
    b_axial = radial_slope + current_field / radius
    eddy_current = -conduct * (current_field - previous)
    force_radial = FORCE_K * eddy_current * b_axial
    force_axial = FORCE_K * eddy_current * axial_slope
    return jnp.concatenate([force_radial[..., 1:-1], force_axial[..., 1:-1]], axis=-1)


def shards(
    coil_density,
    coil_mask,
    drive,
    potential,
    tile_weight,
    relay_owner,
    relay_slot,
    velocity,
    strain,
    plastic,
):
    local_count, axial_cells, radial_cells = potential.shape
    band_width = tile_weight.shape[1]
    azim_total = local_count * lax.axis_size("azim")
    own_index = lax.axis_index("azim") * local_count + jnp.arange(local_count, dtype=jnp.int32)
    band_start = radial_cells // 4
    radius, conduct, coil_zone = radial_profiles(radial_cells, band_start, band_width)
    orders = harmonic_order(own_index, azim_total)
    diagonal_term = (
        4.0 + conduct[None, None, :] + (orders[:, None, None] / radius[None, None, :]) ** 2
    )
    basis = jnp.asarray(basis_constant(azim_total))

    coil = coil_density[..., :band_start] * coil_mask[..., :band_start].astype(jnp.float32)
    field_modes, coil_modes = transform(
        potential.transpose(1, 0, 2), coil.reshape(local_count, -1), basis, inverse=False
    )
    modes = jnp.concatenate(
        [
            field_modes.transpose(1, 0, 2),
            coil_modes.reshape(local_count, axial_cells, band_start),
        ],
        axis=-1,
    )

    reach = STEPS * SWEEPS + 1
    modes = with_halo(modes, (("axial", 1),), reach)
    field_modes = modes[..., :radial_cells]
    coil_modes = jnp.pad(modes[..., radial_cells:], ((0, 0), (0, 0), (0, radial_cells - band_start)))
    span = axial_cells + 2 * reach
    global_z = lax.axis_index("axial") * axial_cells - reach + jnp.arange(span, dtype=jnp.int32)
    inside = ((global_z >= 0) & (global_z < axial_cells * lax.axis_size("axial")))[None, :, None]
    divisor = jnp.where(inside, diagonal_term, jnp.inf)

    weight = harmonic_weight(own_index, azim_total)[:, None, None]
    window = slice(band_start - 1, band_start + band_width + 1)
    iterate = field_modes
    kept = []
    for step_index in range(STEPS):
        right_side = MU_COIL * (drive[step_index] * coil_modes) + conduct * iterate
        for sweep_index in range(SWEEPS):
            axial_pad = jnp.pad(iterate, ((0, 0), (1, 1), (0, 0)))
            nearby = axial_pad[:, 2:] + axial_pad[:, :-2] + radial_sum(iterate)
            iterate = (right_side + nearby) / divisor
        kept.append(iterate[:, reach - 1 : reach + axial_cells + 1] * weight)
    last = kept[-1]
    edges = jnp.concatenate([last[:, :1], last[:, -1:]], axis=1)[..., window]
    pieces = [edges.shape] + [piece[..., window].shape for piece in kept[:-1]]
    extra = jnp.concatenate(
        [edges.reshape(local_count, -1)]
        + [piece[..., window].reshape(local_count, -1) for piece in kept[:-1]],
        axis=1,
    )
    planes, extra = transform(last[:, 1:-1].transpose(1, 0, 2), extra, basis, inverse=True)
    field_out = planes.transpose(1, 0, 2)
    unpacked, offset = [], 0
    for shape in pieces:
        size = math.prod(shape[1:])
        unpacked.append(extra[:, offset : offset + size].reshape(shape))
        offset += size
    edges = unpacked[0]
    fields = unpacked[1:] + [
        jnp.concatenate([edges[:, :1], field_out[..., window], edges[:, 1:]], axis=1)
    ]

    previous = potential[..., window]
    tiles = []
    for step_index in range(STEPS):
        padded = fields[step_index]
        tiles.append(lorentz_window(padded, previous, conduct[window], radius[window]))
        previous = padded[:, 1:-1]
    tiles = jnp.stack(tiles)

    slot_range = jnp.arange(local_count, dtype=jnp.int32)
    slot_table = relay_slot[:, :, 0][:, :, None] == slot_range[None, None, :]
    owner_at = jnp.sum(jnp.where(slot_table, relay_owner[:, :, 0][:, :, None], 0), axis=1)
    moved = jnp.einsum(
        "sjcw,sjp->spcw", tiles, slot_table.astype(jnp.float32), precision=HIGH
    )

    blank = jnp.zeros_like(tile_weight)
    paired = jnp.concatenate(
        [
            jnp.concatenate([tile_weight, blank], axis=2),
            jnp.concatenate([blank, tile_weight], axis=2),
        ],
        axis=1,
    )
    paired = lax.optimization_barrier(paired)
    mapped = jnp.einsum("apr,sazr->sazp", paired, moved, precision=lax.Precision.HIGH)

    def place(target):
        return jnp.where((owner_at == target)[:, :, None, None], mapped, 0.0)

    from_below = shifted(place(2), "axial", 1)
    from_above = shifted(place(0), "axial", -1)
    loads = place(1) + from_below + from_above
    trial_stress = E_MOD * (strain - plastic)
    excess = jnp.abs(trial_stress) - YIELD_ZERO
    increment = (
        trial_stress
        * jnp.maximum(excess, 0.0)
        / ((E_MOD + HARDEN) * jnp.maximum(jnp.abs(trial_stress), YIELD_ZERO))
    )
    plastic = plastic + increment
    stress = E_MOD * (strain - plastic)
    damped, stress = lax.optimization_barrier((DAMPING * velocity, STIFFNESS * stress))
    velocity = damped + TIME_STEP * (loads[0] - stress)
    strain = strain + TIME_STEP * velocity
    for step_index in range(1, STEPS):
        velocity, strain, plastic = plastic_update(loads[step_index], velocity, strain, plastic)
    return (field_out, velocity, strain, plastic)


def solution(mesh):
    placed = (
        P("azim", "axial", None),
        P("azim", "axial", None),
        P(),
        P("azim", "axial", None),
        P("azim", None, None),
        P(None, "azim", "axial"),
        P(None, "azim", "axial"),
        P("azim", "axial", None),
        P("azim", "axial", None),
        P("azim", "axial", None),
    )
    return jax.shard_map(
        shards,
        mesh=mesh,
        in_specs=placed,
        out_specs=(
            P("azim", "axial", None),
            P("azim", "axial", None),
            P("azim", "axial", None),
            P("azim", "axial", None),
        ),
        check_vma=False,
    )
```
